32 devices in a mesh: det: 2 (over x), harm: 16 (over z, y, core).
Axes of the slice: x: 2, y: 2, z: 4, core: 2. Of those that a mesh axis runs over, the one named last changes fastest.
Arguments:
- perturbation: bfloat16 [32, 2, 2, 256, 512], P(('det', 'harm')), parts along dimension 0, may hold values from -16 to 16, as said below
- coupling: bfloat16 [4, 2, 512, 512], replicated, may hold values from -0.1875 to 0.1875
- y_operator: bfloat16 [128, 128], replicated, may hold values from -0.5 to 0.5
- x_operator: bfloat16 [256, 256], replicated, may hold values from -0.5 to 0.5
- tile_mask: int32 [2, 2], replicated, may hold values 0 or 1
- slot_offsets: int32 [4], replicated, may hold values from 0 to 3, each once
- detuning: float32 [2], P('det'), parts along dimension 0, may hold values from -0.5 to 0.5
Outputs:
- image: bfloat16 [32, 2, 2, 256, 512], P(('det', 'harm')), parts along dimension 0
- projected: bfloat16 [32, 2, 2, 256, 512], P(('det', 'harm')), parts along dimension 0
The draws below stay inside these ranges and needn't reach their ends.
There are 2 independent parts, one for each index of `det`. The reference program is written for one: setup_inputs(seed, part) draws one part's arguments, and reference() takes and returns one part's arrays. A program takes and returns all parts, laid end to end along the dimension named above; an argument that names none is the same for every part. Nothing has to cross between parts.
Inputs may be any that keep to these rules, and one draw needn't show every extreme that they name: `perturbation`: real-valued entries with scales that vary over harmonics and streamwise points.
All inputs are finite; a program needn't handle non-finite values.
Results may differ from the reference program's by a relative error of at most 0.0004.
Values may be sent and summed in bfloat16 or wider, within the bound.
No kernel may reach another device: no remote copies, remote signals or barrier semaphores. Data moves between devices by JAX's collectives and lax.ppermute only.
A program may use at most 64 MiB of HBM per device.

```python
import math
import jax
import jax.numpy as jnp
from jax import lax

Y = 128
FY = 512
X = 256
XT = 2
V = 2
SLOTS = 4
HARMONICS = 16


def draw_perturbation(key, part):
    first, second = jax.random.split(jax.random.fold_in(key, 11), 2)
    shape = (HARMONICS, 2, V, X, FY)
    scales = jnp.exp(jax.random.uniform(second, (HARMONICS, 1, 1, X, 1), jnp.float32, math.log(0.4), math.log(4.0)))
    base = jax.random.truncated_normal(first, -4.0, 4.0, shape, jnp.float32)
    return (base * scales).astype(jnp.bfloat16)


def with_ends(values, stream_key, least, high):
    dims = values.shape
    index_at = [jax.random.randint(jax.random.fold_in(stream_key, axis), (), 0, dims[axis]) for axis in range(len(dims))]
    values = values.at[tuple(index_at)].set(least)
    longest = dims.index(max(dims))
    index_at[longest] = (index_at[longest] + 1) % dims[longest]
    return values.at[tuple(index_at)].set(high)


def centred(own_key, shape, scale, bound, kind=jnp.bfloat16):
    return jnp.clip(scale * jax.random.normal(own_key, shape, jnp.float32), -bound, bound).astype(kind)


def setup_inputs(seed: int = 0, part: int = 0) -> dict:
    keys = jax.random.split(jax.random.key(seed), 8)
    part_keys = jax.random.split(jax.random.fold_in(keys[7], part), 8)
    return {
        "perturbation": draw_perturbation(jax.random.fold_in(jax.random.fold_in(keys[7], part), 71), part),
        "coupling": centred(keys[1], (SLOTS, 2, FY, FY), (2 * FY) ** -0.5, 0.1875),
        "y_operator": centred(keys[2], (Y, Y), Y ** -0.5, 0.5),
        "x_operator": centred(keys[3], (X, X), (X // 2) ** -0.5, 0.5),
        "tile_mask": with_ends((jax.random.randint(keys[4], (XT, XT), 0, 2) < 1).astype(jnp.int32), jax.random.fold_in(keys[4], 1), 0, 1),
        "slot_offsets": jax.random.permutation(keys[5], 4).astype(jnp.int32),
        "detuning": jnp.clip(jax.random.uniform(part_keys[6], (1,), jnp.float32, -0.5, 0.5), -0.5, 0.5),
    }


def reference(perturbation, coupling, y_operator, x_operator, tile_mask, slot_offsets, detuning):
    harmonics = perturbation.shape[0]
    vecs = perturbation.shape[2]
    width_x = perturbation.shape[3]
    width_fy = perturbation.shape[4]
    ny = y_operator.shape[0]
    tile = width_x // tile_mask.shape[0]
    full_mask = jnp.repeat(jnp.repeat(tile_mask, tile, axis=0), tile, axis=1)
    masked = (x_operator.astype(jnp.float32) * full_mask.astype(jnp.float32))
    table = jnp.array([-2, -1, 1, 2], dtype=jnp.int32)
    shifts = table[slot_offsets]
    yop = y_operator.astype(jnp.float32)
    coup = coupling.astype(jnp.float32)

    def apply_one(index):
        block = perturbation[index].astype(jnp.float32)
        rows = block.reshape(-1, ny)
        along_y = jnp.dot(rows, yop, preferred_element_type=jnp.float32).reshape(block.shape)
        along_x = jnp.einsum("ab,cvbf->cvaf", masked, block)
        centered = (index - harmonics // 2).astype(jnp.float32) + detuning[0]
        lam = -(centered * centered) / (4.0 * harmonics)
        total = along_y + along_x + lam * block
        for slot in range(4):
            source = jnp.mod(index - shifts[slot], harmonics).astype(jnp.int32)
            other = lax.dynamic_index_in_dim(perturbation, source, 0, keepdims=False).astype(jnp.float32)
            prod = jnp.einsum("cri,kio->ckro", other.reshape(2, vecs * width_x, width_fy), coup[slot])
            real_part = prod[0, 0] - prod[1, 1]
            imag_part = prod[0, 1] + prod[1, 0]
            total = total + jnp.stack([real_part, imag_part]).reshape(block.shape)
        return total

    image = lax.map(apply_one, jnp.arange(harmonics, dtype=jnp.int32))
    qf = perturbation.astype(jnp.float32)
    qr = qf[:, 0]
    qi = qf[:, 1]
    wr = image[:, 0]
    wi = image[:, 1]
    hp = lax.Precision.HIGHEST
    num_re = jnp.einsum("hvxf,huxf->vu", qr, wr, precision=hp) + jnp.einsum("hvxf,huxf->vu", qi, wi, precision=hp)
    num_im = jnp.einsum("hvxf,huxf->vu", qr, wi, precision=hp) - jnp.einsum("hvxf,huxf->vu", qi, wr, precision=hp)
    norms = jnp.sum(qr * qr + qi * qi, axis=(0, 2, 3))
    h_re = num_re / (norms + 1e-6)[:, None]
    h_im = num_im / (norms + 1e-6)[:, None]
    proj_re = wr - jnp.einsum("vu,hvxf->huxf", h_re, qr, precision=hp) + jnp.einsum("vu,hvxf->huxf", h_im, qi, precision=hp)
    proj_im = wi - jnp.einsum("vu,hvxf->huxf", h_re, qi, precision=hp) - jnp.einsum("vu,hvxf->huxf", h_im, qr, precision=hp)
    projected = jnp.stack([proj_re, proj_im], axis=1)
    return image.astype(jnp.bfloat16), projected.astype(jnp.bfloat16)
```

```python
import jax
import jax.numpy as jnp
from jax import lax
from jax.sharding import PartitionSpec as P


def passed_along(value, axis, steps):
    count = lax.axis_size(axis)
    pairs = [(source, (source + steps) % count) for source in range(count)]
    return lax.ppermute(value, axis, pairs)


def summed_over(axes, *parts):
    flat = jnp.concatenate([part.reshape(-1) for part in parts])
    count = 1
    for axis in axes:
        count = count * lax.axis_size(axis)
    spread = jnp.broadcast_to(flat[None], (count,) + flat.shape)
    gathered = lax.all_to_all(spread, axes, 0, 0, tiled=False)
    total = jnp.sum(gathered, axis=0)
    out = []
    start = 0
    for part in parts:
        out.append(total[start:start + part.size].reshape(part.shape))
        start += part.size
    return out


def body(perturbation, coupling, y_operator, x_operator, tile_mask, slot_offsets, detuning):
    block = perturbation[0]
    vecs = block.shape[1]
    width_x = block.shape[2]
    width_fy = block.shape[3]
    ny = y_operator.shape[0]
    harmonics = lax.axis_size("harm")
    position = lax.axis_index("harm")
    tile = width_x // tile_mask.shape[0]
    below_one = passed_along(block, "harm", 1)
    above_one = passed_along(block, "harm", -1)
    below_two = passed_along(below_one, "harm", 1)
    above_two = passed_along(above_one, "harm", -1)
    rows = block.reshape(-1, ny)
    along_y = jnp.dot(rows, y_operator, preferred_element_type=jnp.float32).reshape(block.shape)
    full_mask = jnp.repeat(jnp.repeat(tile_mask, tile, axis=0), tile, axis=1).astype(jnp.bfloat16)
    masked = x_operator * full_mask
    along_x = jnp.einsum("ab,cvbf->cvaf", masked, block, preferred_element_type=jnp.float32)
    centered = (position - harmonics // 2).astype(jnp.float32) + detuning[0]
    lam = -(centered * centered) / (4.0 * harmonics)
    image = along_y + along_x + lam * block.astype(jnp.float32)
    sources = (above_two, above_one, below_one, below_two)
    counter = jnp.arange(4, dtype=jnp.int32)
    for place in range(4):
        slot = jnp.sum(jnp.where(slot_offsets == place, counter, 0))
        matrix = lax.dynamic_index_in_dim(coupling, slot, 0, keepdims=False)
        other = sources[place].reshape(2, vecs * width_x, width_fy)
        prod = jnp.einsum("cri,kio->ckro", other, matrix, preferred_element_type=jnp.float32)
        real_part = prod[0, 0] - prod[1, 1]
        imag_part = prod[0, 1] + prod[1, 0]
        image = image + jnp.stack([real_part, imag_part]).reshape(block.shape)
    hp = lax.Precision.HIGHEST
    qfull = block.astype(jnp.float32)
    qr = qfull[0]
    qi = qfull[1]
    wr = image[0]
    wi = image[1]
    num_re = jnp.einsum("vxf,uxf->vu", qr, wr, precision=hp) + jnp.einsum(
        "vxf,uxf->vu", qi, wi, precision=hp
    )
    num_im = jnp.einsum("vxf,uxf->vu", qr, wi, precision=hp) - jnp.einsum(
        "vxf,uxf->vu", qi, wr, precision=hp
    )
    norms = jnp.sum(qr * qr + qi * qi, axis=(1, 2))
    total_re, total_im, total_norms = summed_over(("harm",), num_re, num_im, norms)
    h_re = total_re / (total_norms + 1e-06)[:, None]
    h_im = total_im / (total_norms + 1e-06)[:, None]
    proj_re = (
        wr
        - jnp.einsum("vu,vxf->uxf", h_re, qr, precision=hp)
        + jnp.einsum("vu,vxf->uxf", h_im, qi, precision=hp)
    )
    proj_im = (
        wi
        - jnp.einsum("vu,vxf->uxf", h_re, qi, precision=hp)
        - jnp.einsum("vu,vxf->uxf", h_im, qr, precision=hp)
    )
    projected = jnp.stack([proj_re, proj_im])
    return (image.astype(jnp.bfloat16)[None], projected.astype(jnp.bfloat16)[None])


def solution(mesh):
    in_specs = (P(("det", "harm"), None, None, None, None), P(), P(), P(), P(), P(), P("det"))
    out_specs = (
        P(("det", "harm"), None, None, None, None),
        P(("det", "harm"), None, None, None, None),
    )
    return jax.shard_map(body, mesh=mesh, in_specs=in_specs, out_specs=out_specs, check_vma=False)
```

```python
import jax
import jax.numpy as jnp
from jax import lax
from jax.sharding import PartitionSpec as P


def passed_along(value, axis, steps):
    count = lax.axis_size(axis)
    pairs = [(source, (source + steps) % count) for source in range(count)]
    return lax.ppermute(value, axis, pairs)


def summed_over(axes, *parts):
    flat = jnp.concatenate([part.reshape(-1) for part in parts])
    count = 1
    for axis in axes:
        count = count * lax.axis_size(axis)
    spread = jnp.broadcast_to(flat[None], (count,) + flat.shape)
    gathered = lax.all_to_all(spread, axes, 0, 0, tiled=False)
    total = jnp.sum(gathered, axis=0)
    out = []
    start = 0
    for part in parts:
        out.append(total[start:start + part.size].reshape(part.shape))
        start += part.size
    return out


def body(perturbation, coupling, y_operator, x_operator, tile_mask, slot_offsets, detuning):
    block = perturbation[0]
    vecs = block.shape[1]
    width_x = block.shape[2]
    width_fy = block.shape[3]
    ny = y_operator.shape[0]
    harmonics = lax.axis_size("harm")
    position = lax.axis_index("harm")
    tile = width_x // tile_mask.shape[0]
    below_one = passed_along(block, "harm", 1)
    above_one = passed_along(block, "harm", -1)
    below_two = passed_along(below_one, "harm", 1)
    above_two = passed_along(above_one, "harm", -1)
    rows = block.reshape(-1, ny)
    along_y = jnp.dot(rows, y_operator, preferred_element_type=jnp.float32).reshape(block.shape)
    full_mask = jnp.repeat(jnp.repeat(tile_mask, tile, axis=0), tile, axis=1).astype(jnp.bfloat16)
    masked = x_operator * full_mask
    along_x = jnp.einsum("ab,cvbf->cvaf", masked, block, preferred_element_type=jnp.float32)
    centered = (position - harmonics // 2).astype(jnp.float32) + detuning[0]
    lam = -(centered * centered) / (4.0 * harmonics)
    image = along_y + along_x + lam * block.astype(jnp.float32)
    sources = (above_two, above_one, below_one, below_two)
    counter = jnp.arange(4, dtype=jnp.int32)
    for place in range(4):
        slot = jnp.sum(jnp.where(slot_offsets == place, counter, 0))
        matrix = lax.dynamic_index_in_dim(coupling, slot, 0, keepdims=False)
        other = sources[place].reshape(2, vecs * width_x, width_fy)
        prod = jnp.einsum("cri,kio->ckro", other, matrix, preferred_element_type=jnp.float32)
        real_part = prod[0, 0] - prod[1, 1]
        imag_part = prod[0, 1] + prod[1, 0]
        image = image + jnp.stack([real_part, imag_part]).reshape(block.shape)
    qfull = block.astype(jnp.float32)
    qr = qfull[0]
    qi = qfull[1]
    wr = image[0]
    wi = image[1]
    num_re = jnp.sum(qr[:, None] * wr[None, :] + qi[:, None] * wi[None, :], axis=(2, 3))
    num_im = jnp.sum(qr[:, None] * wi[None, :] - qi[:, None] * wr[None, :], axis=(2, 3))
    norms = jnp.sum(qr * qr + qi * qi, axis=(1, 2))
    total_re, total_im, total_norms = summed_over(("harm",), num_re, num_im, norms)
    h_re = (total_re / (total_norms + 1e-06)[:, None])[:, :, None, None]
    h_im = (total_im / (total_norms + 1e-06)[:, None])[:, :, None, None]
    proj_re = wr - jnp.sum(h_re * qr[:, None] - h_im * qi[:, None], axis=0)
    proj_im = wi - jnp.sum(h_re * qi[:, None] + h_im * qr[:, None], axis=0)
    projected = jnp.stack([proj_re, proj_im])
    return (image.astype(jnp.bfloat16)[None], projected.astype(jnp.bfloat16)[None])


def solution(mesh):
    in_specs = (P(("det", "harm"), None, None, None, None), P(), P(), P(), P(), P(), P("det"))
    out_specs = (
        P(("det", "harm"), None, None, None, None),
        P(("det", "harm"), None, None, None, None),
    )
    return jax.shard_map(body, mesh=mesh, in_specs=in_specs, out_specs=out_specs, check_vma=False)
```

```python
import jax
import jax.numpy as jnp
from jax import lax
from jax.sharding import PartitionSpec as P


def passed_along(value, axis, steps):
    count = lax.axis_size(axis)
    pairs = [(source, (source + steps) % count) for source in range(count)]
    return lax.ppermute(value, axis, pairs)


def summed_over(axes, *parts):
    flat = jnp.concatenate([part.reshape(-1) for part in parts])
    count = 1
    for axis in axes:
        count = count * lax.axis_size(axis)
    spread = jnp.broadcast_to(flat[None], (count,) + flat.shape)
    gathered = lax.all_to_all(spread, axes, 0, 0, tiled=False)
    total = jnp.sum(gathered, axis=0)
    out = []
    start = 0
    for part in parts:
        out.append(total[start:start + part.size].reshape(part.shape))
        start += part.size
    return out


def body(perturbation, coupling, y_operator, x_operator, tile_mask, slot_offsets, detuning):
    block = perturbation[0]
    vecs = block.shape[1]
    width_x = block.shape[2]
    width_fy = block.shape[3]
    ny = y_operator.shape[0]
    harmonics = lax.axis_size("harm")
    position = lax.axis_index("harm")
    tile = width_x // tile_mask.shape[0]
    below_one = passed_along(block, "harm", 1)
    above_one = passed_along(block, "harm", -1)
    below_two = passed_along(block, "harm", 2)
    above_two = passed_along(block, "harm", -2)
    rows = block.reshape(-1, ny)
    along_y = jnp.dot(rows, y_operator, preferred_element_type=jnp.float32).reshape(block.shape)
    full_mask = jnp.repeat(jnp.repeat(tile_mask, tile, axis=0), tile, axis=1).astype(jnp.bfloat16)
    masked = x_operator * full_mask
    along_x = jnp.einsum("ab,cvbf->cvaf", masked, block, preferred_element_type=jnp.float32)
    centered = (position - harmonics // 2).astype(jnp.float32) + detuning[0]
    lam = -(centered * centered) / (4.0 * harmonics)
    image = along_y + along_x + lam * block.astype(jnp.float32)
    sources = (above_two, above_one, below_one, below_two)
    counter = jnp.arange(4, dtype=jnp.int32)
    for place in range(4):
        slot = jnp.sum(jnp.where(slot_offsets == place, counter, 0))
        matrix = lax.dynamic_index_in_dim(coupling, slot, 0, keepdims=False)
        other = sources[place].reshape(2, vecs * width_x, width_fy)
        prod = jnp.einsum("cri,kio->ckro", other, matrix, preferred_element_type=jnp.float32)
        real_part = prod[0, 0] - prod[1, 1]
        imag_part = prod[0, 1] + prod[1, 0]
        image = image + jnp.stack([real_part, imag_part]).reshape(block.shape)
    qfull = block.astype(jnp.float32)
    qr = qfull[0]
    qi = qfull[1]
    wr = image[0]
    wi = image[1]
    num_re = jnp.sum(qr[:, None] * wr[None, :] + qi[:, None] * wi[None, :], axis=(2, 3))
    num_im = jnp.sum(qr[:, None] * wi[None, :] - qi[:, None] * wr[None, :], axis=(2, 3))
    norms = jnp.sum(qr * qr + qi * qi, axis=(1, 2))
    total_re, total_im, total_norms = summed_over(("harm",), num_re, num_im, norms)
    h_re = (total_re / (total_norms + 1e-06)[:, None])[:, :, None, None]
    h_im = (total_im / (total_norms + 1e-06)[:, None])[:, :, None, None]
    proj_re = wr - jnp.sum(h_re * qr[:, None] - h_im * qi[:, None], axis=0)
    proj_im = wi - jnp.sum(h_re * qi[:, None] + h_im * qr[:, None], axis=0)
    projected = jnp.stack([proj_re, proj_im])
    return (image.astype(jnp.bfloat16)[None], projected.astype(jnp.bfloat16)[None])


def solution(mesh):
    in_specs = (P(("det", "harm"), None, None, None, None), P(), P(), P(), P(), P(), P("det"))
    out_specs = (
        P(("det", "harm"), None, None, None, None),
        P(("det", "harm"), None, None, None, None),
    )
    return jax.shard_map(body, mesh=mesh, in_specs=in_specs, out_specs=out_specs, check_vma=False)
```

```python
import jax
import jax.numpy as jnp
from jax import lax
from jax.sharding import PartitionSpec as P


def passed_along(value, axis, steps, parity=None):
    count = lax.axis_size(axis)
    sources = [source for source in range(count) if parity is None or source % 2 == parity]
    pairs = [(source, (source + steps) % count) for source in sources]
    return lax.ppermute(value, axis, pairs)


def two_away(block, below_one, above_one, axis):
    if lax.axis_size(axis) % 2:
        return passed_along(below_one, axis, 1), passed_along(above_one, axis, -1)
    even = lax.axis_index(axis) % 2 == 0
    far_below = passed_along(block, axis, 2, parity=0)
    near_below = passed_along(below_one, axis, 1, parity=0)
    far_above = passed_along(block, axis, -2, parity=1)
    near_above = passed_along(above_one, axis, -1, parity=1)
    below_two = jnp.where(even, far_below, near_below)
    above_two = jnp.where(even, near_above, far_above)
    return below_two, above_two


def summed_over(axes, *parts):
    flat = jnp.concatenate([part.reshape(-1) for part in parts])
    count = 1
    for axis in axes:
        count = count * lax.axis_size(axis)
    spread = jnp.broadcast_to(flat[None], (count,) + flat.shape)
    gathered = lax.all_to_all(spread, axes, 0, 0, tiled=False)
    total = jnp.sum(gathered, axis=0)
    out = []
    start = 0
    for part in parts:
        out.append(total[start:start + part.size].reshape(part.shape))
        start += part.size
    return out


def body(perturbation, coupling, y_operator, x_operator, tile_mask, slot_offsets, detuning):
    block = perturbation[0]
    vecs = block.shape[1]
    width_x = block.shape[2]
    width_fy = block.shape[3]
    ny = y_operator.shape[0]
    harmonics = lax.axis_size("harm")
    position = lax.axis_index("harm")
    tile = width_x // tile_mask.shape[0]
    below_one = passed_along(block, "harm", 1)
    above_one = passed_along(block, "harm", -1)
    below_two, above_two = two_away(block, below_one, above_one, "harm")
    rows = block.reshape(-1, ny)
    along_y = jnp.dot(rows, y_operator, preferred_element_type=jnp.float32).reshape(block.shape)
    full_mask = jnp.repeat(jnp.repeat(tile_mask, tile, axis=0), tile, axis=1).astype(jnp.bfloat16)
    masked = x_operator * full_mask
    along_x = jnp.einsum("ab,cvbf->cvaf", masked, block, preferred_element_type=jnp.float32)
    centered = (position - harmonics // 2).astype(jnp.float32) + detuning[0]
    lam = -(centered * centered) / (4.0 * harmonics)
    image = along_y + along_x + lam * block.astype(jnp.float32)
    sources = (above_two, above_one, below_one, below_two)
    counter = jnp.arange(4, dtype=jnp.int32)
    for place in range(4):
        slot = jnp.sum(jnp.where(slot_offsets == place, counter, 0))
        matrix = lax.dynamic_index_in_dim(coupling, slot, 0, keepdims=False)
        other = sources[place].reshape(2, vecs * width_x, width_fy)
        prod = jnp.einsum("cri,kio->ckro", other, matrix, preferred_element_type=jnp.float32)
        real_part = prod[0, 0] - prod[1, 1]
        imag_part = prod[0, 1] + prod[1, 0]
        image = image + jnp.stack([real_part, imag_part]).reshape(block.shape)
    qfull = block.astype(jnp.float32)
    qr = qfull[0]
    qi = qfull[1]
    wr = image[0]
    wi = image[1]
    num_re = jnp.sum(qr[:, None] * wr[None, :] + qi[:, None] * wi[None, :], axis=(2, 3))
    num_im = jnp.sum(qr[:, None] * wi[None, :] - qi[:, None] * wr[None, :], axis=(2, 3))
    norms = jnp.sum(qr * qr + qi * qi, axis=(1, 2))
    total_re, total_im, total_norms = summed_over(("harm",), num_re, num_im, norms)
    h_re = (total_re / (total_norms + 1e-06)[:, None])[:, :, None, None]
    h_im = (total_im / (total_norms + 1e-06)[:, None])[:, :, None, None]
    proj_re = wr - jnp.sum(h_re * qr[:, None] - h_im * qi[:, None], axis=0)
    proj_im = wi - jnp.sum(h_re * qi[:, None] + h_im * qr[:, None], axis=0)
    projected = jnp.stack([proj_re, proj_im])
    return (image.astype(jnp.bfloat16)[None], projected.astype(jnp.bfloat16)[None])


def solution(mesh):
    in_specs = (P(("det", "harm"), None, None, None, None), P(), P(), P(), P(), P(), P("det"))
    out_specs = (
        P(("det", "harm"), None, None, None, None),
        P(("det", "harm"), None, None, None, None),
    )
    return jax.shard_map(body, mesh=mesh, in_specs=in_specs, out_specs=out_specs, check_vma=False)
```

```python
import jax
import jax.numpy as jnp
from jax import lax
from jax.sharding import PartitionSpec as P


def passed_along(value, axis, steps):
    count = lax.axis_size(axis)
    pairs = [(source, (source + steps) % count) for source in range(count)]
    return lax.ppermute(value, axis, pairs)


def summed_over(axes, *parts):
    flat = jnp.concatenate([part.reshape(-1) for part in parts])
    count = 1
    for axis in axes:
        count = count * lax.axis_size(axis)
    spread = jnp.broadcast_to(flat[None], (count,) + flat.shape)
    gathered = lax.all_to_all(spread, axes, 0, 0, tiled=False)
    total = jnp.sum(gathered, axis=0)
    out = []
    start = 0
    for part in parts:
        out.append(total[start:start + part.size].reshape(part.shape))
        start += part.size
    return out


def body(perturbation, coupling, y_operator, x_operator, tile_mask, slot_offsets, detuning):
    block = perturbation[0]
    vecs = block.shape[1]
    width_x = block.shape[2]
    width_fy = block.shape[3]
    ny = y_operator.shape[0]
    harmonics = lax.axis_size("harm")
    position = lax.axis_index("harm")
    tile = width_x // tile_mask.shape[0]
    pieces = 2 if width_x % 16 == 0 else 1
    chunks = jnp.split(block, pieces, axis=2)
    ones_below = [passed_along(chunk, "harm", 1) for chunk in chunks]
    ones_above = [passed_along(chunk, "harm", -1) for chunk in chunks]
    twos_below = [passed_along(chunk, "harm", 1) for chunk in ones_below]
    twos_above = [passed_along(chunk, "harm", -1) for chunk in ones_above]
    rows = block.reshape(-1, ny)
    along_y = jnp.dot(rows, y_operator, preferred_element_type=jnp.float32).reshape(block.shape)
    full_mask = jnp.repeat(jnp.repeat(tile_mask, tile, axis=0), tile, axis=1).astype(jnp.bfloat16)
    masked = x_operator * full_mask
    along_x = jnp.einsum("ab,cvbf->cvaf", masked, block, preferred_element_type=jnp.float32)
    centered = (position - harmonics // 2).astype(jnp.float32) + detuning[0]
    lam = -(centered * centered) / (4.0 * harmonics)
    image = along_y + along_x + lam * block.astype(jnp.float32)
    sources = (twos_above, ones_above, ones_below, twos_below)
    counter = jnp.arange(4, dtype=jnp.int32)
    coupled = [None] * pieces
    for place in range(4):
        slot = jnp.sum(jnp.where(slot_offsets == place, counter, 0))
        matrix = lax.dynamic_index_in_dim(coupling, slot, 0, keepdims=False)
        for piece in range(pieces):
            other = sources[place][piece]
            rows_shape = other.shape
            other = other.reshape(2, -1, width_fy)
            prod = jnp.einsum("cri,kio->ckro", other, matrix, preferred_element_type=jnp.float32)
            real_part = prod[0, 0] - prod[1, 1]
            imag_part = prod[0, 1] + prod[1, 0]
            term = jnp.stack([real_part, imag_part]).reshape(rows_shape)
            coupled[piece] = term if coupled[piece] is None else coupled[piece] + term
    image = image + jnp.concatenate(coupled, axis=2)
    qfull = block.astype(jnp.float32)
    qr = qfull[0]
    qi = qfull[1]
    wr = image[0]
    wi = image[1]
    num_re = jnp.sum(qr[:, None] * wr[None, :] + qi[:, None] * wi[None, :], axis=(2, 3))
    num_im = jnp.sum(qr[:, None] * wi[None, :] - qi[:, None] * wr[None, :], axis=(2, 3))
    norms = jnp.sum(qr * qr + qi * qi, axis=(1, 2))
    total_re, total_im, total_norms = summed_over(("harm",), num_re, num_im, norms)
    h_re = (total_re / (total_norms + 1e-06)[:, None])[:, :, None, None]
    h_im = (total_im / (total_norms + 1e-06)[:, None])[:, :, None, None]
    proj_re = wr - jnp.sum(h_re * qr[:, None] - h_im * qi[:, None], axis=0)
    proj_im = wi - jnp.sum(h_re * qi[:, None] + h_im * qr[:, None], axis=0)
    projected = jnp.stack([proj_re, proj_im])
    return (image.astype(jnp.bfloat16)[None], projected.astype(jnp.bfloat16)[None])


def solution(mesh):
    in_specs = (P(("det", "harm"), None, None, None, None), P(), P(), P(), P(), P(), P("det"))
    out_specs = (
        P(("det", "harm"), None, None, None, None),
        P(("det", "harm"), None, None, None, None),
    )
    return jax.shard_map(body, mesh=mesh, in_specs=in_specs, out_specs=out_specs, check_vma=False)
```

```python
import jax
import jax.numpy as jnp
from jax import lax
from jax.sharding import PartitionSpec as P


def passed_along(value, axis, steps):
    count = lax.axis_size(axis)
    pairs = [(source, (source + steps) % count) for source in range(count)]
    return lax.ppermute(value, axis, pairs)


def summed_over(axes, *parts):
    flat = jnp.concatenate([part.reshape(-1) for part in parts])
    count = 1
    for axis in axes:
        count = count * lax.axis_size(axis)
    spread = jnp.broadcast_to(flat[None], (count,) + flat.shape)
    gathered = lax.all_to_all(spread, axes, 0, 0, tiled=False)
    total = jnp.sum(gathered, axis=0)
    out = []
    start = 0
    for part in parts:
        out.append(total[start:start + part.size].reshape(part.shape))
        start += part.size
    return out


def body(perturbation, coupling, y_operator, x_operator, tile_mask, slot_offsets, detuning):
    block = perturbation[0]
    vecs = block.shape[1]
    width_x = block.shape[2]
    width_fy = block.shape[3]
    ny = y_operator.shape[0]
    harmonics = lax.axis_size("harm")
    position = lax.axis_index("harm")
    tile = width_x // tile_mask.shape[0]
    below_one = passed_along(block, "harm", 1)
    above_one = passed_along(block, "harm", -1)
    block, below_one, above_one = lax.optimization_barrier((block, below_one, above_one))
    below_two = passed_along(below_one, "harm", 1)
    above_two = passed_along(above_one, "harm", -1)
    rows = block.reshape(-1, ny)
    along_y = jnp.dot(rows, y_operator, preferred_element_type=jnp.float32).reshape(block.shape)
    full_mask = jnp.repeat(jnp.repeat(tile_mask, tile, axis=0), tile, axis=1).astype(jnp.bfloat16)
    masked = x_operator * full_mask
    along_x = jnp.einsum("ab,cvbf->cvaf", masked, block, preferred_element_type=jnp.float32)
    centered = (position - harmonics // 2).astype(jnp.float32) + detuning[0]
    lam = -(centered * centered) / (4.0 * harmonics)
    image = along_y + along_x + lam * block.astype(jnp.float32)
    sources = (above_two, above_one, below_one, below_two)
    counter = jnp.arange(4, dtype=jnp.int32)
    for place in range(4):
        slot = jnp.sum(jnp.where(slot_offsets == place, counter, 0))
        matrix = lax.dynamic_index_in_dim(coupling, slot, 0, keepdims=False)
        other = sources[place].reshape(2, vecs * width_x, width_fy)
        prod = jnp.einsum("cri,kio->ckro", other, matrix, preferred_element_type=jnp.float32)
        real_part = prod[0, 0] - prod[1, 1]
        imag_part = prod[0, 1] + prod[1, 0]
        image = image + jnp.stack([real_part, imag_part]).reshape(block.shape)
    qfull = block.astype(jnp.float32)
    qr = qfull[0]
    qi = qfull[1]
    wr = image[0]
    wi = image[1]
    num_re = jnp.sum(qr[:, None] * wr[None, :] + qi[:, None] * wi[None, :], axis=(2, 3))
    num_im = jnp.sum(qr[:, None] * wi[None, :] - qi[:, None] * wr[None, :], axis=(2, 3))
    norms = jnp.sum(qr * qr + qi * qi, axis=(1, 2))
    total_re, total_im, total_norms = summed_over(("harm",), num_re, num_im, norms)
    h_re = (total_re / (total_norms + 1e-06)[:, None])[:, :, None, None]
    h_im = (total_im / (total_norms + 1e-06)[:, None])[:, :, None, None]
    proj_re = wr - jnp.sum(h_re * qr[:, None] - h_im * qi[:, None], axis=0)
    proj_im = wi - jnp.sum(h_re * qi[:, None] + h_im * qr[:, None], axis=0)
    projected = jnp.stack([proj_re, proj_im])
    return (image.astype(jnp.bfloat16)[None], projected.astype(jnp.bfloat16)[None])


def solution(mesh):
    in_specs = (P(("det", "harm"), None, None, None, None), P(), P(), P(), P(), P(), P("det"))
    out_specs = (
        P(("det", "harm"), None, None, None, None),
        P(("det", "harm"), None, None, None, None),
    )
    return jax.shard_map(body, mesh=mesh, in_specs=in_specs, out_specs=out_specs, check_vma=False)
```

```python
import jax
import jax.numpy as jnp
from jax import lax
from jax.sharding import PartitionSpec as P


def passed_along(value, axis, steps):
    count = lax.axis_size(axis)
    pairs = [(source, (source + steps) % count) for source in range(count)]
    return lax.ppermute(value, axis, pairs)


def summed_over(axes, *parts):
    flat = jnp.concatenate([part.reshape(-1) for part in parts])
    count = 1
    for axis in axes:
        count = count * lax.axis_size(axis)
    spread = jnp.broadcast_to(flat[None], (count,) + flat.shape)
    gathered = lax.all_to_all(spread, axes, 0, 0, tiled=False)
    total = jnp.sum(gathered, axis=0)
    out = []
    start = 0
    for part in parts:
        out.append(total[start:start + part.size].reshape(part.shape))
        start += part.size
    return out


def body(perturbation, coupling, y_operator, x_operator, tile_mask, slot_offsets, detuning):
    block = perturbation[0]
    vecs = block.shape[1]
    width_x = block.shape[2]
    width_fy = block.shape[3]
    ny = y_operator.shape[0]
    harmonics = lax.axis_size("harm")
    position = lax.axis_index("harm")
    tile = width_x // tile_mask.shape[0]
    below_one = passed_along(block, "harm", 1)
    above_one = passed_along(block, "harm", -1)
    below_two = passed_along(below_one, "harm", 1)
    above_two = passed_along(above_one, "harm", -1)
    rows = block.reshape(-1, ny)
    along_y = jnp.dot(rows, y_operator, preferred_element_type=jnp.float32).reshape(block.shape)
    full_mask = jnp.repeat(jnp.repeat(tile_mask, tile, axis=0), tile, axis=1).astype(jnp.bfloat16)
    masked = x_operator * full_mask
    along_x = jnp.einsum("ab,cvbf->cvaf", masked, block, preferred_element_type=jnp.float32)
    centered = (position - harmonics // 2).astype(jnp.float32) + detuning[0]
    lam = -(centered * centered) / (4.0 * harmonics)
    qfull = block.astype(jnp.float32)
    qr = qfull[0]
    qi = qfull[1]

    def products(term):
        tr = term[0]
        ti = term[1]
        part_re = jnp.sum(qr[:, None] * tr[None, :] + qi[:, None] * ti[None, :], axis=(2, 3))
        part_im = jnp.sum(qr[:, None] * ti[None, :] - qi[:, None] * tr[None, :], axis=(2, 3))
        return part_re, part_im

    image = along_y + along_x + lam * qfull
    num_re, num_im = products(image)
    sources = (above_two, above_one, below_one, below_two)
    counter = jnp.arange(4, dtype=jnp.int32)
    for place in range(4):
        slot = jnp.sum(jnp.where(slot_offsets == place, counter, 0))
        matrix = lax.dynamic_index_in_dim(coupling, slot, 0, keepdims=False)
        other = sources[place].reshape(2, vecs * width_x, width_fy)
        prod = jnp.einsum("cri,kio->ckro", other, matrix, preferred_element_type=jnp.float32)
        real_part = prod[0, 0] - prod[1, 1]
        imag_part = prod[0, 1] + prod[1, 0]
        term = jnp.stack([real_part, imag_part]).reshape(block.shape)
        part_re, part_im = products(term)
        num_re = num_re + part_re
        num_im = num_im + part_im
        image = image + term
    wr = image[0]
    wi = image[1]
    norms = jnp.sum(qr * qr + qi * qi, axis=(1, 2))
    total_re, total_im, total_norms = summed_over(("harm",), num_re, num_im, norms)
    h_re = (total_re / (total_norms + 1e-06)[:, None])[:, :, None, None]
    h_im = (total_im / (total_norms + 1e-06)[:, None])[:, :, None, None]
    proj_re = wr - jnp.sum(h_re * qr[:, None] - h_im * qi[:, None], axis=0)
    proj_im = wi - jnp.sum(h_re * qi[:, None] + h_im * qr[:, None], axis=0)
    projected = jnp.stack([proj_re, proj_im])
    return (image.astype(jnp.bfloat16)[None], projected.astype(jnp.bfloat16)[None])


def solution(mesh):
    in_specs = (P(("det", "harm"), None, None, None, None), P(), P(), P(), P(), P(), P("det"))
    out_specs = (
        P(("det", "harm"), None, None, None, None),
        P(("det", "harm"), None, None, None, None),
    )
    return jax.shard_map(body, mesh=mesh, in_specs=in_specs, out_specs=out_specs, check_vma=False)
```

```python
import jax
import jax.numpy as jnp
from jax import lax
from jax.sharding import PartitionSpec as P


def passed_along(value, axis, steps):
    count = lax.axis_size(axis)
    pairs = [(source, (source + steps) % count) for source in range(count)]
    return lax.ppermute(value, axis, pairs)


def summed_over(axes, *parts):
    flat = jnp.concatenate([part.reshape(-1) for part in parts])
    count = 1
    for axis in axes:
        count = count * lax.axis_size(axis)
    spread = jnp.broadcast_to(flat[None], (count,) + flat.shape)
    gathered = lax.all_to_all(spread, axes, 0, 0, tiled=False)
    total = jnp.sum(gathered, axis=0)
    out = []
    start = 0
    for part in parts:
        out.append(total[start:start + part.size].reshape(part.shape))
        start += part.size
    return out


def body(perturbation, coupling, y_operator, x_operator, tile_mask, slot_offsets, detuning):
    block = perturbation[0]
    parts, vecs, width_x, width_fy = block.shape
    ny = y_operator.shape[0]
    harmonics = lax.axis_size("harm")
    position = lax.axis_index("harm")
    tile = width_x // tile_mask.shape[0]
    below_one = passed_along(block, "harm", 1)
    above_one = passed_along(block, "harm", -1)
    below_two = passed_along(below_one, "harm", 1)
    above_two = passed_along(above_one, "harm", -1)
    rows = block.reshape(-1, ny)
    along_y = jnp.dot(rows, y_operator, preferred_element_type=jnp.float32).reshape(block.shape)
    full_mask = jnp.repeat(jnp.repeat(tile_mask, tile, axis=0), tile, axis=1).astype(jnp.bfloat16)
    masked = x_operator * full_mask
    planes = block.reshape(parts * vecs, width_x, width_fy)
    spread = jnp.broadcast_to(masked, (parts * vecs,) + masked.shape)
    along_x = jnp.einsum("nab,nbf->naf", spread, planes, preferred_element_type=jnp.float32)
    centered = (position - harmonics // 2).astype(jnp.float32) + detuning[0]
    lam = -(centered * centered) / (4.0 * harmonics)
    qfull = block.astype(jnp.float32)
    image = along_y + along_x.reshape(block.shape) + lam * qfull
    sources = (above_two, above_one, below_one, below_two)
    counter = jnp.arange(4, dtype=jnp.int32)
    for place in range(4):
        slot = jnp.sum(jnp.where(slot_offsets == place, counter, 0))
        matrix = lax.dynamic_index_in_dim(coupling, slot, 0, keepdims=False)
        real_form = jnp.stack([jnp.stack([matrix[0], matrix[1]]), jnp.stack([-matrix[1], matrix[0]])])
        other = sources[place].reshape(parts, vecs * width_x, width_fy)
        term = jnp.einsum("cri,cdio->dro", other, real_form, preferred_element_type=jnp.float32)
        image = image + term.reshape(block.shape)
    turned = jnp.stack([-qfull[1], qfull[0]])
    num_re = jnp.sum(qfull[:, :, None] * image[:, None], axis=(0, 3, 4))
    num_im = jnp.sum(turned[:, :, None] * image[:, None], axis=(0, 3, 4))
    norms = jnp.sum(qfull * qfull, axis=(0, 2, 3))
    total_re, total_im, total_norms = summed_over(("harm",), num_re, num_im, norms)
    h_re = (total_re / (total_norms + 1e-06)[:, None])[None, :, :, None, None]
    h_im = (total_im / (total_norms + 1e-06)[:, None])[None, :, :, None, None]
    projected = image - jnp.sum(h_re * qfull[:, :, None] + h_im * turned[:, :, None], axis=1)
    return (image.astype(jnp.bfloat16)[None], projected.astype(jnp.bfloat16)[None])


def solution(mesh):
    in_specs = (P(("det", "harm"), None, None, None, None), P(), P(), P(), P(), P(), P("det"))
    out_specs = (
        P(("det", "harm"), None, None, None, None),
        P(("det", "harm"), None, None, None, None),
    )
    return jax.shard_map(body, mesh=mesh, in_specs=in_specs, out_specs=out_specs, check_vma=False)
```

```python
import jax
import jax.numpy as jnp
from jax import lax
from jax.sharding import PartitionSpec as P


def passed_along(value, axis, steps):
    count = lax.axis_size(axis)
    pairs = [(source, (source + steps) % count) for source in range(count)]
    return lax.ppermute(value, axis, pairs)


def summed_over(axes, *parts):
    flat = jnp.concatenate([part.reshape(-1) for part in parts])
    count = 1
    for axis in axes:
        count = count * lax.axis_size(axis)
    spread = jnp.broadcast_to(flat[None], (count,) + flat.shape)
    gathered = lax.all_to_all(spread, axes, 0, 0, tiled=False)
    total = jnp.sum(gathered, axis=0)
    out = []
    start = 0
    for part in parts:
        out.append(total[start:start + part.size].reshape(part.shape))
        start += part.size
    return out


def body(perturbation, coupling, y_operator, x_operator, tile_mask, slot_offsets, detuning):
    block = perturbation[0]
    vecs = block.shape[1]
    width_x = block.shape[2]
    width_fy = block.shape[3]
    ny = y_operator.shape[0]
    harmonics = lax.axis_size("harm")
    position = lax.axis_index("harm")
    tile = width_x // tile_mask.shape[0]
    below_one = passed_along(block, "harm", 1)
    above_one = passed_along(block, "harm", -1)
    below_two = passed_along(below_one, "harm", 1)
    above_two = passed_along(above_one, "harm", -1)
    rows = block.reshape(-1, ny)
    along_y = jnp.dot(rows, y_operator, preferred_element_type=jnp.float32).reshape(block.shape)
    full_mask = jnp.repeat(jnp.repeat(tile_mask, tile, axis=0), tile, axis=1).astype(jnp.bfloat16)
    masked = x_operator * full_mask
    along_x = jnp.einsum("ab,cvbf->cvaf", masked, block, preferred_element_type=jnp.float32)
    centered = (position - harmonics // 2).astype(jnp.float32) + detuning[0]
    lam = -(centered * centered) / (4.0 * harmonics)
    image = along_y + along_x + lam * block.astype(jnp.float32)
    sources = (above_two, above_one, below_one, below_two)
    counter = jnp.arange(4, dtype=jnp.int32)
    for place in range(4):
        slot = jnp.sum(jnp.where(slot_offsets == place, counter, 0))
        matrix = lax.dynamic_index_in_dim(coupling, slot, 0, keepdims=False)
        other = sources[place].reshape(2, vecs * width_x, width_fy)
        prod = jnp.einsum("cri,kio->ckro", other, matrix, preferred_element_type=jnp.float32)
        real_part = prod[0, 0] - prod[1, 1]
        imag_part = prod[0, 1] + prod[1, 0]
        image = image + jnp.stack([real_part, imag_part]).reshape(block.shape)
    qfull = block.astype(jnp.float32)
    qr = qfull[0]
    qi = qfull[1]
    wr = image[0]
    wi = image[1]
    num_re = jnp.sum(qr[:, None] * wr[None, :] + qi[:, None] * wi[None, :], axis=(2, 3))
    num_im = jnp.sum(qr[:, None] * wi[None, :] - qi[:, None] * wr[None, :], axis=(2, 3))
    norms = jnp.sum(qr * qr + qi * qi, axis=(1, 2))
    total_re, total_im, total_norms = summed_over(("harm",), num_re, num_im, norms)
    h_re = total_re / (total_norms + 1e-06)[:, None]
    h_im = total_im / (total_norms + 1e-06)[:, None]
    turned = jnp.stack([-qi, qr])
    projected = image
    for vec in range(vecs):
        projected = projected - (h_re[vec, :, None, None] * qfull[:, vec][:, None]
                                 + h_im[vec, :, None, None] * turned[:, vec][:, None])
    return (image.astype(jnp.bfloat16)[None], projected.astype(jnp.bfloat16)[None])


def solution(mesh):
    in_specs = (P(("det", "harm"), None, None, None, None), P(), P(), P(), P(), P(), P("det"))
    out_specs = (
        P(("det", "harm"), None, None, None, None),
        P(("det", "harm"), None, None, None, None),
    )
    return jax.shard_map(body, mesh=mesh, in_specs=in_specs, out_specs=out_specs, check_vma=False)
```

```python
import jax
import jax.numpy as jnp
from jax import lax
from jax.sharding import PartitionSpec as P


def passed_along(value, axis, steps):
    count = lax.axis_size(axis)
    pairs = [(source, (source + steps) % count) for source in range(count)]
    return lax.ppermute(value, axis, pairs)


def summed_over(axes, *parts):
    flat = jnp.concatenate([part.reshape(-1) for part in parts])
    count = 1
    for axis in axes:
        count = count * lax.axis_size(axis)
    spread = jnp.broadcast_to(flat[None], (count,) + flat.shape)
    gathered = lax.all_to_all(spread, axes, 0, 0, tiled=False)
    total = jnp.sum(gathered, axis=0)
    out = []
    start = 0
    for part in parts:
        out.append(total[start:start + part.size].reshape(part.shape))
        start += part.size
    return out


def body(perturbation, coupling, y_operator, x_operator, tile_mask, slot_offsets, detuning):
    block = perturbation[0]
    vecs = block.shape[1]
    width_x = block.shape[2]
    width_fy = block.shape[3]
    ny = y_operator.shape[0]
    harmonics = lax.axis_size("harm")
    position = lax.axis_index("harm")
    tile = width_x // tile_mask.shape[0]
    below_one = passed_along(block, "harm", 1)
    above_one = passed_along(block, "harm", -1)
    below_two = passed_along(below_one, "harm", 1)
    above_two = passed_along(above_one, "harm", -1)
    rows = block.reshape(-1, ny)
    along_y = jnp.dot(rows, y_operator, preferred_element_type=jnp.float32).reshape(block.shape)
    full_mask = jnp.repeat(jnp.repeat(tile_mask, tile, axis=0), tile, axis=1).astype(jnp.bfloat16)
    masked = x_operator * full_mask
    planes = block.reshape(-1, width_x, width_fy)
    spread = jnp.broadcast_to(masked, (planes.shape[0],) + masked.shape)
    along_x = jnp.einsum("nab,nbf->naf", spread, planes, preferred_element_type=jnp.float32)
    along_x = along_x.reshape(block.shape)
    centered = (position - harmonics // 2).astype(jnp.float32) + detuning[0]
    lam = -(centered * centered) / (4.0 * harmonics)
    image = along_y + along_x + lam * block.astype(jnp.float32)
    sources = (above_two, above_one, below_one, below_two)
    counter = jnp.arange(4, dtype=jnp.int32)
    for place in range(4):
        slot = jnp.sum(jnp.where(slot_offsets == place, counter, 0))
        matrix = lax.dynamic_index_in_dim(coupling, slot, 0, keepdims=False)
        other = sources[place].reshape(2, vecs * width_x, width_fy)
        prod = jnp.einsum("cri,kio->ckro", other, matrix, preferred_element_type=jnp.float32)
        real_part = prod[0, 0] - prod[1, 1]
        imag_part = prod[0, 1] + prod[1, 0]
        image = image + jnp.stack([real_part, imag_part]).reshape(block.shape)
    qfull = block.astype(jnp.float32)
    qr = qfull[0]
    qi = qfull[1]
    wr = image[0]
    wi = image[1]
    num_re = jnp.sum(qr[:, None] * wr[None, :] + qi[:, None] * wi[None, :], axis=(2, 3))
    num_im = jnp.sum(qr[:, None] * wi[None, :] - qi[:, None] * wr[None, :], axis=(2, 3))
    norms = jnp.sum(qr * qr + qi * qi, axis=(1, 2))
    total_re, total_im, total_norms = summed_over(("harm",), num_re, num_im, norms)
    h_re = total_re / (total_norms + 1e-06)[:, None]
    h_im = total_im / (total_norms + 1e-06)[:, None]
    turned = jnp.stack([-qi, qr])
    projected = image
    for vec in range(vecs):
        projected = projected - (h_re[vec, :, None, None] * qfull[:, vec][:, None]
                                 + h_im[vec, :, None, None] * turned[:, vec][:, None])
    return (image.astype(jnp.bfloat16)[None], projected.astype(jnp.bfloat16)[None])


def solution(mesh):
    in_specs = (P(("det", "harm"), None, None, None, None), P(), P(), P(), P(), P(), P("det"))
    out_specs = (
        P(("det", "harm"), None, None, None, None),
        P(("det", "harm"), None, None, None, None),
    )
    return jax.shard_map(body, mesh=mesh, in_specs=in_specs, out_specs=out_specs, check_vma=False)
```

```python
import jax
import jax.numpy as jnp
from jax import lax
from jax.experimental import pallas as pl
from jax.experimental.pallas import tpu as pltpu
from jax.sharding import PartitionSpec as P


def passed_along(value, axis, steps):
    count = lax.axis_size(axis)
    pairs = [(source, (source + steps) % count) for source in range(count)]
    return lax.ppermute(value, axis, pairs)


def summed_over(axes, *parts):
    flat = jnp.concatenate([part.reshape(-1) for part in parts])
    count = 1
    for axis in axes:
        count = count * lax.axis_size(axis)
    spread = jnp.broadcast_to(flat[None], (count,) + flat.shape)
    gathered = lax.all_to_all(spread, axes, 0, 0, tiled=False)
    total = jnp.sum(gathered, axis=0)
    out = []
    start = 0
    for part in parts:
        out.append(total[start:start + part.size].reshape(part.shape))
        start += part.size
    return out


def body(perturbation, coupling, y_operator, x_operator, tile_mask, slot_offsets, detuning):
    block = perturbation[0]
    vecs = block.shape[1]
    width_x = block.shape[2]
    width_fy = block.shape[3]
    ny = y_operator.shape[0]
    harmonics = lax.axis_size("harm")
    position = lax.axis_index("harm")
    tile = width_x // tile_mask.shape[0]
    below_one = passed_along(block, "harm", 1)
    above_one = passed_along(block, "harm", -1)
    below_two = passed_along(below_one, "harm", 1)
    above_two = passed_along(above_one, "harm", -1)
    rows = block.reshape(-1, ny)
    along_y = jnp.dot(rows, y_operator, preferred_element_type=jnp.float32).reshape(block.shape)
    full_mask = jnp.repeat(jnp.repeat(tile_mask, tile, axis=0), tile, axis=1).astype(jnp.bfloat16)
    masked = x_operator * full_mask
    along_x = jnp.einsum("ab,cvbf->cvaf", masked, block, preferred_element_type=jnp.float32)
    centered = (position - harmonics // 2).astype(jnp.float32) + detuning[0]
    lam = -(centered * centered) / (4.0 * harmonics)
    image = along_y + along_x + lam * block.astype(jnp.float32)
    sources = (above_two, above_one, below_one, below_two)
    counter = jnp.arange(4, dtype=jnp.int32)
    for place in range(4):
        slot = jnp.sum(jnp.where(slot_offsets == place, counter, 0))
        matrix = lax.dynamic_index_in_dim(coupling, slot, 0, keepdims=False)
        other = sources[place].reshape(2, vecs * width_x, width_fy)
        prod = jnp.einsum("cri,kio->ckro", other, matrix, preferred_element_type=jnp.float32)
        real_part = prod[0, 0] - prod[1, 1]
        imag_part = prod[0, 1] + prod[1, 0]
        image = image + jnp.stack([real_part, imag_part]).reshape(block.shape)
    qfull = block.astype(jnp.float32)
    qr = qfull[0]
    qi = qfull[1]
    wr = image[0]
    wi = image[1]
    num_re = jnp.sum(qr[:, None] * wr[None, :] + qi[:, None] * wi[None, :], axis=(2, 3))
    num_im = jnp.sum(qr[:, None] * wi[None, :] - qi[:, None] * wr[None, :], axis=(2, 3))
    norms = jnp.sum(qr * qr + qi * qi, axis=(1, 2))
    total_re, total_im, total_norms = summed_over(("harm",), num_re, num_im, norms)
    h_re = total_re / (total_norms + 1e-06)[:, None]
    h_im = total_im / (total_norms + 1e-06)[:, None]
    weights = jnp.concatenate([h_re.reshape(-1), h_im.reshape(-1)])
    projected = removed_projections(weights, image, perturbation)
    return (image.astype(jnp.bfloat16)[None], projected)


def project_kernel(weights_ref, image_ref, block_ref, out_ref):
    vecs = image_ref.shape[1]
    block = block_ref[0].astype(jnp.float32)
    for u in range(vecs):
        out_re = image_ref[0, u]
        out_im = image_ref[1, u]
        for v in range(vecs):
            a = weights_ref[v * vecs + u]
            b = weights_ref[vecs * vecs + v * vecs + u]
            q_re = block[0, v]
            q_im = block[1, v]
            out_re = out_re - (a * q_re - b * q_im)
            out_im = out_im - (a * q_im + b * q_re)
        out_ref[0, 0, u] = out_re.astype(out_ref.dtype)
        out_ref[0, 1, u] = out_im.astype(out_ref.dtype)


def removed_projections(weights, image, perturbation):
    parts, vecs, width_x, width_fy = image.shape
    rows = 64 if width_x % 64 == 0 else width_x
    return pl.pallas_call(
        project_kernel,
        grid=(width_x // rows,),
        in_specs=[
            pl.BlockSpec(memory_space=pltpu.SMEM),
            pl.BlockSpec((parts, vecs, rows, width_fy), lambda i: (0, 0, i, 0)),
            pl.BlockSpec((1, parts, vecs, rows, width_fy), lambda i: (0, 0, 0, i, 0)),
        ],
        out_specs=pl.BlockSpec((1, parts, vecs, rows, width_fy), lambda i: (0, 0, 0, i, 0)),
        out_shape=jax.ShapeDtypeStruct(perturbation.shape, jnp.bfloat16),
    )(weights, image, perturbation)


def solution(mesh):
    in_specs = (P(("det", "harm"), None, None, None, None), P(), P(), P(), P(), P(), P("det"))
    out_specs = (
        P(("det", "harm"), None, None, None, None),
        P(("det", "harm"), None, None, None, None),
    )
    return jax.shard_map(body, mesh=mesh, in_specs=in_specs, out_specs=out_specs, check_vma=False)
```

```python
import jax
import jax.numpy as jnp
from jax import lax
from jax.experimental import pallas as pl
from jax.experimental.pallas import tpu as pltpu
from jax.sharding import PartitionSpec as P


def passed_along(value, axis, steps):
    count = lax.axis_size(axis)
    pairs = [(source, (source + steps) % count) for source in range(count)]
    return lax.ppermute(value, axis, pairs)


def summed_over(axes, *parts):
    flat = jnp.concatenate([part.reshape(-1) for part in parts])
    count = 1
    for axis in axes:
        count = count * lax.axis_size(axis)
    spread = jnp.broadcast_to(flat[None], (count,) + flat.shape)
    gathered = lax.all_to_all(spread, axes, 0, 0, tiled=False)
    total = jnp.sum(gathered, axis=0)
    out = []
    start = 0
    for part in parts:
        out.append(total[start:start + part.size].reshape(part.shape))
        start += part.size
    return out


def body(perturbation, coupling, y_operator, x_operator, tile_mask, slot_offsets, detuning):
    block = perturbation[0]
    vecs = block.shape[1]
    width_x = block.shape[2]
    width_fy = block.shape[3]
    ny = y_operator.shape[0]
    harmonics = lax.axis_size("harm")
    position = lax.axis_index("harm")
    tile = width_x // tile_mask.shape[0]
    below_one = passed_along(block, "harm", 1)
    above_one = passed_along(block, "harm", -1)
    below_two = passed_along(below_one, "harm", 1)
    above_two = passed_along(above_one, "harm", -1)
    rows = block.reshape(-1, ny)
    along_y = jnp.dot(rows, y_operator, preferred_element_type=jnp.float32).reshape(block.shape)
    full_mask = jnp.repeat(jnp.repeat(tile_mask, tile, axis=0), tile, axis=1).astype(jnp.bfloat16)
    masked = x_operator * full_mask
    along_x = jnp.einsum("ab,cvbf->cvaf", masked, block, preferred_element_type=jnp.float32)
    centered = (position - harmonics // 2).astype(jnp.float32) + detuning[0]
    lam = -(centered * centered) / (4.0 * harmonics)
    image = along_y + along_x + lam * block.astype(jnp.float32)
    sources = (above_two, above_one, below_one, below_two)
    counter = jnp.arange(4, dtype=jnp.int32)
    for place in range(4):
        slot = jnp.sum(jnp.where(slot_offsets == place, counter, 0))
        matrix = lax.dynamic_index_in_dim(coupling, slot, 0, keepdims=False)
        other = sources[place].reshape(2, vecs * width_x, width_fy)
        prod = jnp.einsum("cri,kio->ckro", other, matrix, preferred_element_type=jnp.float32)
        real_part = prod[0, 0] - prod[1, 1]
        imag_part = prod[0, 1] + prod[1, 0]
        image = image + jnp.stack([real_part, imag_part]).reshape(block.shape)
    qfull = block.astype(jnp.float32)
    qr = qfull[0]
    qi = qfull[1]
    wr = image[0]
    wi = image[1]
    num_re = jnp.sum(qr[:, None] * wr[None, :] + qi[:, None] * wi[None, :], axis=(2, 3))
    num_im = jnp.sum(qr[:, None] * wi[None, :] - qi[:, None] * wr[None, :], axis=(2, 3))
    norms = jnp.sum(qr * qr + qi * qi, axis=(1, 2))
    total_re, total_im, total_norms = summed_over(("harm",), num_re, num_im, norms)
    h_re = total_re / (total_norms + 1e-06)[:, None]
    h_im = total_im / (total_norms + 1e-06)[:, None]
    projected = removed_projections(h_re.reshape(-1), h_im.reshape(-1), image, perturbation)
    return (image.astype(jnp.bfloat16)[None], projected)


def project_kernel(real_ref, imag_ref, image_ref, block_ref, out_ref):
    vecs = image_ref.shape[1]
    block = block_ref[0].astype(jnp.float32)
    for u in range(vecs):
        out_re = image_ref[0, u]
        out_im = image_ref[1, u]
        for v in range(vecs):
            a = real_ref[v * vecs + u]
            b = imag_ref[v * vecs + u]
            q_re = block[0, v]
            q_im = block[1, v]
            out_re = out_re - (a * q_re - b * q_im)
            out_im = out_im - (a * q_im + b * q_re)
        out_ref[0, 0, u] = out_re.astype(out_ref.dtype)
        out_ref[0, 1, u] = out_im.astype(out_ref.dtype)


def removed_projections(real, imag, image, perturbation):
    parts, vecs, width_x, width_fy = image.shape
    rows = 128 if width_x % 128 == 0 else width_x
    return pl.pallas_call(
        project_kernel,
        grid=(width_x // rows,),
        in_specs=[
            pl.BlockSpec(memory_space=pltpu.SMEM),
            pl.BlockSpec(memory_space=pltpu.SMEM),
            pl.BlockSpec((parts, vecs, rows, width_fy), lambda i: (0, 0, i, 0)),
            pl.BlockSpec((1, parts, vecs, rows, width_fy), lambda i: (0, 0, 0, i, 0)),
        ],
        out_specs=pl.BlockSpec((1, parts, vecs, rows, width_fy), lambda i: (0, 0, 0, i, 0)),
        out_shape=jax.ShapeDtypeStruct(perturbation.shape, jnp.bfloat16),
    )(real, imag, image, perturbation)


def solution(mesh):
    in_specs = (P(("det", "harm"), None, None, None, None), P(), P(), P(), P(), P(), P("det"))
    out_specs = (
        P(("det", "harm"), None, None, None, None),
        P(("det", "harm"), None, None, None, None),
    )
    return jax.shard_map(body, mesh=mesh, in_specs=in_specs, out_specs=out_specs, check_vma=False)
```

```python
import jax
import jax.numpy as jnp
from jax import lax
from jax.experimental import pallas as pl
from jax.experimental.pallas import tpu as pltpu
from jax.sharding import PartitionSpec as P


def passed_along(value, axis, steps):
    count = lax.axis_size(axis)
    pairs = [(source, (source + steps) % count) for source in range(count)]
    return lax.ppermute(value, axis, pairs)


def exchanged(axes, *parts):
    count = 1
    for axis in axes:
        count = count * lax.axis_size(axis)
    spread = jnp.concatenate([jnp.broadcast_to(part.reshape(1, -1), (count, part.size)) for part in parts], axis=1)
    return lax.all_to_all(spread, axes, 0, 0, tiled=True)


def body(perturbation, coupling, y_operator, x_operator, tile_mask, slot_offsets, detuning):
    block = perturbation[0]
    vecs = block.shape[1]
    width_x = block.shape[2]
    width_fy = block.shape[3]
    ny = y_operator.shape[0]
    harmonics = lax.axis_size("harm")
    position = lax.axis_index("harm")
    tile = width_x // tile_mask.shape[0]
    below_one = passed_along(block, "harm", 1)
    above_one = passed_along(block, "harm", -1)
    below_two = passed_along(below_one, "harm", 1)
    above_two = passed_along(above_one, "harm", -1)
    rows = block.reshape(-1, ny)
    along_y = jnp.dot(rows, y_operator, preferred_element_type=jnp.float32).reshape(block.shape)
    full_mask = jnp.repeat(jnp.repeat(tile_mask, tile, axis=0), tile, axis=1).astype(jnp.bfloat16)
    masked = x_operator * full_mask
    along_x = jnp.einsum("ab,cvbf->cvaf", masked, block, preferred_element_type=jnp.float32)
    centered = (position - harmonics // 2).astype(jnp.float32) + detuning[0]
    lam = -(centered * centered) / (4.0 * harmonics)
    image = along_y + along_x + lam * block.astype(jnp.float32)
    sources = (above_two, above_one, below_one, below_two)
    counter = jnp.arange(4, dtype=jnp.int32)
    for place in range(4):
        slot = jnp.sum(jnp.where(slot_offsets == place, counter, 0))
        matrix = lax.dynamic_index_in_dim(coupling, slot, 0, keepdims=False)
        other = sources[place].reshape(2, vecs * width_x, width_fy)
        prod = jnp.einsum("cri,kio->ckro", other, matrix, preferred_element_type=jnp.float32)
        real_part = prod[0, 0] - prod[1, 1]
        imag_part = prod[0, 1] + prod[1, 0]
        image = image + jnp.stack([real_part, imag_part]).reshape(block.shape)
    qfull = block.astype(jnp.float32)
    qr = qfull[0]
    qi = qfull[1]
    wr = image[0]
    wi = image[1]
    num_re = jnp.sum(qr[:, None] * wr[None, :] + qi[:, None] * wi[None, :], axis=(2, 3))
    num_im = jnp.sum(qr[:, None] * wi[None, :] - qi[:, None] * wr[None, :], axis=(2, 3))
    norms = jnp.sum(qr * qr + qi * qi, axis=(1, 2))
    gathered = exchanged(("harm",), num_re, num_im, norms)
    projected = removed_projections(gathered, image, perturbation)
    return (image.astype(jnp.bfloat16)[None], projected)


def project_kernel(gathered_ref, image_ref, block_ref, out_ref):
    vecs = image_ref.shape[1]
    count, values = gathered_ref.shape
    totals = []
    for j in range(values):
        total = gathered_ref[0, j]
        for i in range(1, count):
            total = total + gathered_ref[i, j]
        totals.append(total)
    block = block_ref[0].astype(jnp.float32)
    for u in range(vecs):
        out_re = image_ref[0, u]
        out_im = image_ref[1, u]
        for v in range(vecs):
            scale = jnp.full((1, 1), totals[2 * vecs * vecs + v] + 1e-06, jnp.float32)
            a = jnp.full((1, 1), totals[v * vecs + u], jnp.float32) / scale
            b = jnp.full((1, 1), totals[vecs * vecs + v * vecs + u], jnp.float32) / scale
            q_re = block[0, v]
            q_im = block[1, v]
            out_re = out_re - (a * q_re - b * q_im)
            out_im = out_im - (a * q_im + b * q_re)
        out_ref[0, 0, u] = out_re.astype(out_ref.dtype)
        out_ref[0, 1, u] = out_im.astype(out_ref.dtype)


def removed_projections(gathered, image, perturbation):
    parts, vecs, width_x, width_fy = image.shape
    rows = 128 if width_x % 128 == 0 else width_x
    return pl.pallas_call(
        project_kernel,
        grid=(width_x // rows,),
        in_specs=[
            pl.BlockSpec(memory_space=pltpu.SMEM),
            pl.BlockSpec((parts, vecs, rows, width_fy), lambda i: (0, 0, i, 0)),
            pl.BlockSpec((1, parts, vecs, rows, width_fy), lambda i: (0, 0, 0, i, 0)),
        ],
        out_specs=pl.BlockSpec((1, parts, vecs, rows, width_fy), lambda i: (0, 0, 0, i, 0)),
        out_shape=jax.ShapeDtypeStruct(perturbation.shape, jnp.bfloat16),
    )(gathered, image, perturbation)


def solution(mesh):
    in_specs = (P(("det", "harm"), None, None, None, None), P(), P(), P(), P(), P(), P("det"))
    out_specs = (
        P(("det", "harm"), None, None, None, None),
        P(("det", "harm"), None, None, None, None),
    )
    return jax.shard_map(body, mesh=mesh, in_specs=in_specs, out_specs=out_specs, check_vma=False)
```

```python
import jax
import jax.numpy as jnp
from jax import lax
from jax.experimental import pallas as pl
from jax.experimental.pallas import tpu as pltpu
from jax.sharding import PartitionSpec as P


def passed_along(value, axis, steps):
    count = lax.axis_size(axis)
    pairs = [(source, (source + steps) % count) for source in range(count)]
    return lax.ppermute(value, axis, pairs)


def summed_over(axis, *parts):
    flat = jnp.concatenate([part.reshape(1, -1) for part in parts], axis=1)
    count = lax.axis_size(axis)
    if count & (count - 1) == 0:
        step = 1
        while step < count:
            flat = flat + lax.ppermute(flat, axis, [(i, i ^ step) for i in range(count)])
            step *= 2
        return flat
    spread = jnp.broadcast_to(flat, (count, flat.shape[1]))
    gathered = lax.all_to_all(spread, axis, 0, 0, tiled=True)
    return jnp.sum(gathered, axis=0, keepdims=True)


def body(perturbation, coupling, y_operator, x_operator, tile_mask, slot_offsets, detuning):
    block = perturbation[0]
    vecs = block.shape[1]
    width_x = block.shape[2]
    width_fy = block.shape[3]
    ny = y_operator.shape[0]
    harmonics = lax.axis_size("harm")
    position = lax.axis_index("harm")
    tile = width_x // tile_mask.shape[0]
    below_one = passed_along(block, "harm", 1)
    above_one = passed_along(block, "harm", -1)
    below_two = passed_along(below_one, "harm", 1)
    above_two = passed_along(above_one, "harm", -1)
    rows = block.reshape(-1, ny)
    along_y = jnp.dot(rows, y_operator, preferred_element_type=jnp.float32).reshape(block.shape)
    full_mask = jnp.repeat(jnp.repeat(tile_mask, tile, axis=0), tile, axis=1).astype(jnp.bfloat16)
    masked = x_operator * full_mask
    along_x = jnp.einsum("ab,cvbf->cvaf", masked, block, preferred_element_type=jnp.float32)
    centered = (position - harmonics // 2).astype(jnp.float32) + detuning[0]
    lam = -(centered * centered) / (4.0 * harmonics)
    image = along_y + along_x + lam * block.astype(jnp.float32)
    sources = (above_two, above_one, below_one, below_two)
    counter = jnp.arange(4, dtype=jnp.int32)
    for place in range(4):
        slot = jnp.sum(jnp.where(slot_offsets == place, counter, 0))
        matrix = lax.dynamic_index_in_dim(coupling, slot, 0, keepdims=False)
        other = sources[place].reshape(2, vecs * width_x, width_fy)
        prod = jnp.einsum("cri,kio->ckro", other, matrix, preferred_element_type=jnp.float32)
        real_part = prod[0, 0] - prod[1, 1]
        imag_part = prod[0, 1] + prod[1, 0]
        image = image + jnp.stack([real_part, imag_part]).reshape(block.shape)
    qfull = block.astype(jnp.float32)
    qr = qfull[0]
    qi = qfull[1]
    wr = image[0]
    wi = image[1]
    num_re = jnp.sum(qr[:, None] * wr[None, :] + qi[:, None] * wi[None, :], axis=(2, 3))
    num_im = jnp.sum(qr[:, None] * wi[None, :] - qi[:, None] * wr[None, :], axis=(2, 3))
    norms = jnp.sum(qr * qr + qi * qi, axis=(1, 2))
    gathered = summed_over("harm", num_re, num_im, norms)
    projected = removed_projections(gathered, image, perturbation)
    return (image.astype(jnp.bfloat16)[None], projected)


def project_kernel(gathered_ref, image_ref, block_ref, out_ref):
    vecs = image_ref.shape[1]
    count, values = gathered_ref.shape
    totals = []
    for j in range(values):
        total = gathered_ref[0, j]
        for i in range(1, count):
            total = total + gathered_ref[i, j]
        totals.append(total)
    block = block_ref[0].astype(jnp.float32)
    for u in range(vecs):
        out_re = image_ref[0, u]
        out_im = image_ref[1, u]
        for v in range(vecs):
            scale = jnp.full((1, 1), totals[2 * vecs * vecs + v] + 1e-06, jnp.float32)
            a = jnp.full((1, 1), totals[v * vecs + u], jnp.float32) / scale
            b = jnp.full((1, 1), totals[vecs * vecs + v * vecs + u], jnp.float32) / scale
            q_re = block[0, v]
            q_im = block[1, v]
            out_re = out_re - (a * q_re - b * q_im)
            out_im = out_im - (a * q_im + b * q_re)
        out_ref[0, 0, u] = out_re.astype(out_ref.dtype)
        out_ref[0, 1, u] = out_im.astype(out_ref.dtype)


def removed_projections(gathered, image, perturbation):
    parts, vecs, width_x, width_fy = image.shape
    rows = 128 if width_x % 128 == 0 else width_x
    return pl.pallas_call(
        project_kernel,
        grid=(width_x // rows,),
        in_specs=[
            pl.BlockSpec(memory_space=pltpu.SMEM),
            pl.BlockSpec((parts, vecs, rows, width_fy), lambda i: (0, 0, i, 0)),
            pl.BlockSpec((1, parts, vecs, rows, width_fy), lambda i: (0, 0, 0, i, 0)),
        ],
        out_specs=pl.BlockSpec((1, parts, vecs, rows, width_fy), lambda i: (0, 0, 0, i, 0)),
        out_shape=jax.ShapeDtypeStruct(perturbation.shape, jnp.bfloat16),
    )(gathered, image, perturbation)


def solution(mesh):
    in_specs = (P(("det", "harm"), None, None, None, None), P(), P(), P(), P(), P(), P("det"))
    out_specs = (
        P(("det", "harm"), None, None, None, None),
        P(("det", "harm"), None, None, None, None),
    )
    return jax.shard_map(body, mesh=mesh, in_specs=in_specs, out_specs=out_specs, check_vma=False)
```

```python
import jax
import jax.numpy as jnp
from jax import lax
from jax.experimental import pallas as pl
from jax.experimental.pallas import tpu as pltpu
from jax.sharding import PartitionSpec as P


def passed_along(value, axis, steps, parity=None):
    count = lax.axis_size(axis)
    sources = [source for source in range(count) if parity is None or source % 2 == parity]
    pairs = [(source, (source + steps) % count) for source in sources]
    return lax.ppermute(value, axis, pairs)


def neighbours(block, axis):
    if lax.axis_size(axis) % 2:
        below_one = passed_along(block, axis, 1)
        above_one = passed_along(block, axis, -1)
        return below_one, above_one, passed_along(below_one, axis, 1), passed_along(above_one, axis, -1)
    even = lax.axis_index(axis) % 2 == 0
    near_up = passed_along(block, axis, 1, parity=0)
    far_up = passed_along(block, axis, 1, parity=1)
    near_down = passed_along(block, axis, -1, parity=1)
    far_down = passed_along(block, axis, -1, parity=0)
    far_up_two = passed_along(near_up, axis, 1, parity=1)
    far_down_two = passed_along(near_down, axis, -1, parity=0)
    near_up_two = passed_along(far_up, axis, 1, parity=0)
    near_down_two = passed_along(far_down, axis, -1, parity=1)
    below_one = jnp.where(even, far_up, near_up)
    above_one = jnp.where(even, near_down, far_down)
    below_two = jnp.where(even, far_up_two, near_up_two)
    above_two = jnp.where(even, near_down_two, far_down_two)
    return below_one, above_one, below_two, above_two


def exchanged(axes, *parts):
    count = 1
    for axis in axes:
        count = count * lax.axis_size(axis)
    spread = jnp.concatenate([jnp.broadcast_to(part.reshape(1, -1), (count, part.size)) for part in parts], axis=1)
    return lax.all_to_all(spread, axes, 0, 0, tiled=True)


def body(perturbation, coupling, y_operator, x_operator, tile_mask, slot_offsets, detuning):
    block = perturbation[0]
    vecs = block.shape[1]
    width_x = block.shape[2]
    width_fy = block.shape[3]
    ny = y_operator.shape[0]
    harmonics = lax.axis_size("harm")
    position = lax.axis_index("harm")
    tile = width_x // tile_mask.shape[0]
    below_one, above_one, below_two, above_two = neighbours(block, "harm")
    rows = block.reshape(-1, ny)
    along_y = jnp.dot(rows, y_operator, preferred_element_type=jnp.float32).reshape(block.shape)
    full_mask = jnp.repeat(jnp.repeat(tile_mask, tile, axis=0), tile, axis=1).astype(jnp.bfloat16)
    masked = x_operator * full_mask
    along_x = jnp.einsum("ab,cvbf->cvaf", masked, block, preferred_element_type=jnp.float32)
    centered = (position - harmonics // 2).astype(jnp.float32) + detuning[0]
    lam = -(centered * centered) / (4.0 * harmonics)
    image = along_y + along_x + lam * block.astype(jnp.float32)
    sources = (above_two, above_one, below_one, below_two)
    counter = jnp.arange(4, dtype=jnp.int32)
    for place in range(4):
        slot = jnp.sum(jnp.where(slot_offsets == place, counter, 0))
        matrix = lax.dynamic_index_in_dim(coupling, slot, 0, keepdims=False)
        other = sources[place].reshape(2, vecs * width_x, width_fy)
        prod = jnp.einsum("cri,kio->ckro", other, matrix, preferred_element_type=jnp.float32)
        real_part = prod[0, 0] - prod[1, 1]
        imag_part = prod[0, 1] + prod[1, 0]
        image = image + jnp.stack([real_part, imag_part]).reshape(block.shape)
    qfull = block.astype(jnp.float32)
    qr = qfull[0]
    qi = qfull[1]
    wr = image[0]
    wi = image[1]
    num_re = jnp.sum(qr[:, None] * wr[None, :] + qi[:, None] * wi[None, :], axis=(2, 3))
    num_im = jnp.sum(qr[:, None] * wi[None, :] - qi[:, None] * wr[None, :], axis=(2, 3))
    norms = jnp.sum(qr * qr + qi * qi, axis=(1, 2))
    gathered = exchanged(("harm",), num_re, num_im, norms)
    projected = removed_projections(gathered, image, perturbation)
    return (image.astype(jnp.bfloat16)[None], projected)


def project_kernel(gathered_ref, image_ref, block_ref, out_ref):
    vecs = image_ref.shape[1]
    count, values = gathered_ref.shape
    totals = []
    for j in range(values):
        total = gathered_ref[0, j]
        for i in range(1, count):
            total = total + gathered_ref[i, j]
        totals.append(total)
    block = block_ref[0].astype(jnp.float32)
    for u in range(vecs):
        out_re = image_ref[0, u]
        out_im = image_ref[1, u]
        for v in range(vecs):
            scale = jnp.full((1, 1), totals[2 * vecs * vecs + v] + 1e-06, jnp.float32)
            a = jnp.full((1, 1), totals[v * vecs + u], jnp.float32) / scale
            b = jnp.full((1, 1), totals[vecs * vecs + v * vecs + u], jnp.float32) / scale
            q_re = block[0, v]
            q_im = block[1, v]
            out_re = out_re - (a * q_re - b * q_im)
            out_im = out_im - (a * q_im + b * q_re)
        out_ref[0, 0, u] = out_re.astype(out_ref.dtype)
        out_ref[0, 1, u] = out_im.astype(out_ref.dtype)


def removed_projections(gathered, image, perturbation):
    parts, vecs, width_x, width_fy = image.shape
    rows = 128 if width_x % 128 == 0 else width_x
    return pl.pallas_call(
        project_kernel,
        grid=(width_x // rows,),
        in_specs=[
            pl.BlockSpec(memory_space=pltpu.SMEM),
            pl.BlockSpec((parts, vecs, rows, width_fy), lambda i: (0, 0, i, 0)),
            pl.BlockSpec((1, parts, vecs, rows, width_fy), lambda i: (0, 0, 0, i, 0)),
        ],
        out_specs=pl.BlockSpec((1, parts, vecs, rows, width_fy), lambda i: (0, 0, 0, i, 0)),
        out_shape=jax.ShapeDtypeStruct(perturbation.shape, jnp.bfloat16),
    )(gathered, image, perturbation)


def solution(mesh):
    in_specs = (P(("det", "harm"), None, None, None, None), P(), P(), P(), P(), P(), P("det"))
    out_specs = (
        P(("det", "harm"), None, None, None, None),
        P(("det", "harm"), None, None, None, None),
    )
    return jax.shard_map(body, mesh=mesh, in_specs=in_specs, out_specs=out_specs, check_vma=False)
```

```python
import jax
import jax.numpy as jnp
from jax import lax
from jax.experimental import pallas as pl
from jax.experimental.pallas import tpu as pltpu
from jax.sharding import PartitionSpec as P


def passed_along(value, axis, steps):
    count = lax.axis_size(axis)
    pairs = [(source, (source + steps) % count) for source in range(count)]
    return lax.ppermute(value, axis, pairs)


def exchanged(axes, *parts):
    count = 1
    for axis in axes:
        count = count * lax.axis_size(axis)
    spread = jnp.concatenate([jnp.broadcast_to(part.reshape(1, -1), (count, part.size)) for part in parts], axis=1)
    return lax.all_to_all(spread, axes, 0, 0, tiled=True)


def body(perturbation, coupling, y_operator, x_operator, tile_mask, slot_offsets, detuning):
    block = perturbation[0]
    vecs = block.shape[1]
    width_x = block.shape[2]
    width_fy = block.shape[3]
    ny = y_operator.shape[0]
    harmonics = lax.axis_size("harm")
    position = lax.axis_index("harm")
    tile = width_x // tile_mask.shape[0]
    below_one = passed_along(block, "harm", 1)
    above_one = passed_along(block, "harm", -1)
    below_one, above_one = lax.optimization_barrier((below_one, above_one))
    below_two = passed_along(below_one, "harm", 1)
    above_two = passed_along(above_one, "harm", -1)
    rows = block.reshape(-1, ny)
    along_y = jnp.dot(rows, y_operator, preferred_element_type=jnp.float32).reshape(block.shape)
    full_mask = jnp.repeat(jnp.repeat(tile_mask, tile, axis=0), tile, axis=1).astype(jnp.bfloat16)
    masked = x_operator * full_mask
    along_x = jnp.einsum("ab,cvbf->cvaf", masked, block, preferred_element_type=jnp.float32)
    centered = (position - harmonics // 2).astype(jnp.float32) + detuning[0]
    lam = -(centered * centered) / (4.0 * harmonics)
    image = along_y + along_x + lam * block.astype(jnp.float32)
    sources = (above_two, above_one, below_one, below_two)
    counter = jnp.arange(4, dtype=jnp.int32)
    for place in range(4):
        slot = jnp.sum(jnp.where(slot_offsets == place, counter, 0))
        matrix = lax.dynamic_index_in_dim(coupling, slot, 0, keepdims=False)
        other = sources[place].reshape(2, vecs * width_x, width_fy)
        prod = jnp.einsum("cri,kio->ckro", other, matrix, preferred_element_type=jnp.float32)
        real_part = prod[0, 0] - prod[1, 1]
        imag_part = prod[0, 1] + prod[1, 0]
        image = image + jnp.stack([real_part, imag_part]).reshape(block.shape)
    qfull = block.astype(jnp.float32)
    qr = qfull[0]
    qi = qfull[1]
    wr = image[0]
    wi = image[1]
    num_re = jnp.sum(qr[:, None] * wr[None, :] + qi[:, None] * wi[None, :], axis=(2, 3))
    num_im = jnp.sum(qr[:, None] * wi[None, :] - qi[:, None] * wr[None, :], axis=(2, 3))
    norms = jnp.sum(qr * qr + qi * qi, axis=(1, 2))
    gathered = exchanged(("harm",), num_re, num_im, norms)
    projected = removed_projections(gathered, image, perturbation)
    return (image.astype(jnp.bfloat16)[None], projected)


def project_kernel(gathered_ref, image_ref, block_ref, out_ref):
    vecs = image_ref.shape[1]
    count, values = gathered_ref.shape
    totals = []
    for j in range(values):
        total = gathered_ref[0, j]
        for i in range(1, count):
            total = total + gathered_ref[i, j]
        totals.append(total)
    block = block_ref[0].astype(jnp.float32)
    for u in range(vecs):
        out_re = image_ref[0, u]
        out_im = image_ref[1, u]
        for v in range(vecs):
            scale = jnp.full((1, 1), totals[2 * vecs * vecs + v] + 1e-06, jnp.float32)
            a = jnp.full((1, 1), totals[v * vecs + u], jnp.float32) / scale
            b = jnp.full((1, 1), totals[vecs * vecs + v * vecs + u], jnp.float32) / scale
            q_re = block[0, v]
            q_im = block[1, v]
            out_re = out_re - (a * q_re - b * q_im)
            out_im = out_im - (a * q_im + b * q_re)
        out_ref[0, 0, u] = out_re.astype(out_ref.dtype)
        out_ref[0, 1, u] = out_im.astype(out_ref.dtype)


def removed_projections(gathered, image, perturbation):
    parts, vecs, width_x, width_fy = image.shape
    rows = 128 if width_x % 128 == 0 else width_x
    return pl.pallas_call(
        project_kernel,
        grid=(width_x // rows,),
        in_specs=[
            pl.BlockSpec(memory_space=pltpu.SMEM),
            pl.BlockSpec((parts, vecs, rows, width_fy), lambda i: (0, 0, i, 0)),
            pl.BlockSpec((1, parts, vecs, rows, width_fy), lambda i: (0, 0, 0, i, 0)),
        ],
        out_specs=pl.BlockSpec((1, parts, vecs, rows, width_fy), lambda i: (0, 0, 0, i, 0)),
        out_shape=jax.ShapeDtypeStruct(perturbation.shape, jnp.bfloat16),
    )(gathered, image, perturbation)


def solution(mesh):
    in_specs = (P(("det", "harm"), None, None, None, None), P(), P(), P(), P(), P(), P("det"))
    out_specs = (
        P(("det", "harm"), None, None, None, None),
        P(("det", "harm"), None, None, None, None),
    )
    return jax.shard_map(body, mesh=mesh, in_specs=in_specs, out_specs=out_specs, check_vma=False)
```

```python
import jax
import jax.numpy as jnp
from jax import lax
from jax.experimental import pallas as pl
from jax.experimental.pallas import tpu as pltpu
from jax.sharding import PartitionSpec as P


def passed_along(value, axis, steps):
    count = lax.axis_size(axis)
    pairs = [(source, (source + steps) % count) for source in range(count)]
    return lax.ppermute(value, axis, pairs)


def exchanged(axes, *parts):
    count = 1
    for axis in axes:
        count = count * lax.axis_size(axis)
    spread = jnp.concatenate([jnp.broadcast_to(part.reshape(1, -1), (count, part.size)) for part in parts], axis=1)
    return lax.all_to_all(spread, axes, 0, 0, tiled=True)


def body(perturbation, coupling, y_operator, x_operator, tile_mask, slot_offsets, detuning):
    block = perturbation[0]
    vecs = block.shape[1]
    width_x = block.shape[2]
    width_fy = block.shape[3]
    ny = y_operator.shape[0]
    harmonics = lax.axis_size("harm")
    position = lax.axis_index("harm")
    tile = width_x // tile_mask.shape[0]
    below_one = passed_along(block, "harm", 1)
    above_one = passed_along(block, "harm", -1)
    below_two = passed_along(below_one, "harm", 1)
    above_two = passed_along(above_one, "harm", -1)
    rows = block.reshape(-1, ny)
    along_y = jnp.dot(rows, y_operator, preferred_element_type=jnp.float32).reshape(block.shape)
    full_mask = jnp.repeat(jnp.repeat(tile_mask, tile, axis=0), tile, axis=1).astype(jnp.bfloat16)
    masked = x_operator * full_mask
    along_x = jnp.einsum("ab,cvbf->cvaf", masked, block, preferred_element_type=jnp.float32)
    centered = (position - harmonics // 2).astype(jnp.float32) + detuning[0]
    lam = -(centered * centered) / (4.0 * harmonics)
    qfull = block.astype(jnp.float32)
    qr = qfull[0]
    qi = qfull[1]
    image = along_y + along_x + lam * qfull
    num_re = jnp.sum(qr[:, None] * image[0][None, :] + qi[:, None] * image[1][None, :], axis=(2, 3))
    num_im = jnp.sum(qr[:, None] * image[1][None, :] - qi[:, None] * image[0][None, :], axis=(2, 3))
    flat = block.reshape(2, vecs * width_x, width_fy)
    sources = (above_two, above_one, below_one, below_two)
    counter = jnp.arange(4, dtype=jnp.int32)
    for place in range(4):
        slot = jnp.sum(jnp.where(slot_offsets == place, counter, 0))
        matrix = lax.dynamic_index_in_dim(coupling, slot, 0, keepdims=False)
        back = jnp.einsum("cro,kio->ckri", flat, matrix, preferred_element_type=jnp.float32)
        pull_a = (back[0, 0] + back[1, 1]).reshape(vecs, width_x, width_fy)
        pull_b = (back[1, 0] - back[0, 1]).reshape(vecs, width_x, width_fy)
        source = sources[place]
        s_re = source[0].astype(jnp.float32)
        s_im = source[1].astype(jnp.float32)
        num_re = num_re + jnp.sum(pull_a[:, None] * s_re[None, :] + pull_b[:, None] * s_im[None, :], axis=(2, 3))
        num_im = num_im + jnp.sum(pull_a[:, None] * s_im[None, :] - pull_b[:, None] * s_re[None, :], axis=(2, 3))
        other = source.reshape(2, vecs * width_x, width_fy)
        prod = jnp.einsum("cri,kio->ckro", other, matrix, preferred_element_type=jnp.float32)
        real_part = prod[0, 0] - prod[1, 1]
        imag_part = prod[0, 1] + prod[1, 0]
        image = image + jnp.stack([real_part, imag_part]).reshape(block.shape)
    norms = jnp.sum(qr * qr + qi * qi, axis=(1, 2))
    gathered = exchanged(("harm",), num_re, num_im, norms)
    projected = removed_projections(gathered, image, perturbation)
    return (image.astype(jnp.bfloat16)[None], projected)


def project_kernel(gathered_ref, image_ref, block_ref, out_ref):
    vecs = image_ref.shape[1]
    count, values = gathered_ref.shape
    totals = []
    for j in range(values):
        total = gathered_ref[0, j]
        for i in range(1, count):
            total = total + gathered_ref[i, j]
        totals.append(total)
    block = block_ref[0].astype(jnp.float32)
    for u in range(vecs):
        out_re = image_ref[0, u]
        out_im = image_ref[1, u]
        for v in range(vecs):
            scale = jnp.full((1, 1), totals[2 * vecs * vecs + v] + 1e-06, jnp.float32)
            a = jnp.full((1, 1), totals[v * vecs + u], jnp.float32) / scale
            b = jnp.full((1, 1), totals[vecs * vecs + v * vecs + u], jnp.float32) / scale
            q_re = block[0, v]
            q_im = block[1, v]
            out_re = out_re - (a * q_re - b * q_im)
            out_im = out_im - (a * q_im + b * q_re)
        out_ref[0, 0, u] = out_re.astype(out_ref.dtype)
        out_ref[0, 1, u] = out_im.astype(out_ref.dtype)


def removed_projections(gathered, image, perturbation):
    parts, vecs, width_x, width_fy = image.shape
    rows = 128 if width_x % 128 == 0 else width_x
    return pl.pallas_call(
        project_kernel,
        grid=(width_x // rows,),
        in_specs=[
            pl.BlockSpec(memory_space=pltpu.SMEM),
            pl.BlockSpec((parts, vecs, rows, width_fy), lambda i: (0, 0, i, 0)),
            pl.BlockSpec((1, parts, vecs, rows, width_fy), lambda i: (0, 0, 0, i, 0)),
        ],
        out_specs=pl.BlockSpec((1, parts, vecs, rows, width_fy), lambda i: (0, 0, 0, i, 0)),
        out_shape=jax.ShapeDtypeStruct(perturbation.shape, jnp.bfloat16),
    )(gathered, image, perturbation)


def solution(mesh):
    in_specs = (P(("det", "harm"), None, None, None, None), P(), P(), P(), P(), P(), P("det"))
    out_specs = (
        P(("det", "harm"), None, None, None, None),
        P(("det", "harm"), None, None, None, None),
    )
    return jax.shard_map(body, mesh=mesh, in_specs=in_specs, out_specs=out_specs, check_vma=False)
```

```python
import jax
import jax.numpy as jnp
from jax import lax
from jax.experimental import pallas as pl
from jax.experimental.pallas import tpu as pltpu
from jax.sharding import PartitionSpec as P


def passed_along(value, axis, steps):
    count = lax.axis_size(axis)
    pairs = [(source, (source + steps) % count) for source in range(count)]
    return lax.ppermute(value, axis, pairs)


def exchanged(axes, *parts):
    count = 1
    for axis in axes:
        count = count * lax.axis_size(axis)
    spread = jnp.concatenate([jnp.broadcast_to(part.reshape(1, -1), (count, part.size)) for part in parts], axis=1)
    return lax.all_to_all(spread, axes, 0, 0, tiled=True)


def body(perturbation, coupling, y_operator, x_operator, tile_mask, slot_offsets, detuning):
    block = perturbation[0]
    vecs = block.shape[1]
    width_x = block.shape[2]
    width_fy = block.shape[3]
    ny = y_operator.shape[0]
    harmonics = lax.axis_size("harm")
    position = lax.axis_index("harm")
    tile = width_x // tile_mask.shape[0]
    below_one = passed_along(block, "harm", 1)
    above_one = passed_along(block, "harm", -1)
    below_two = passed_along(below_one, "harm", 1)
    above_two = passed_along(above_one, "harm", -1)
    rows = block.reshape(-1, ny)
    along_y = jnp.dot(rows, y_operator, preferred_element_type=jnp.float32).reshape(block.shape)
    full_mask = jnp.repeat(jnp.repeat(tile_mask, tile, axis=0), tile, axis=1).astype(jnp.bfloat16)
    masked = x_operator * full_mask
    along_x = jnp.einsum("ab,cvbf->cvaf", masked, block, preferred_element_type=jnp.float32)
    centered = (position - harmonics // 2).astype(jnp.float32) + detuning[0]
    lam = -(centered * centered) / (4.0 * harmonics)
    image = along_y + along_x + lam * block.astype(jnp.float32)
    sources = (above_two, above_one, below_one, below_two)
    counter = jnp.arange(4, dtype=jnp.int32)
    terms = []
    for place in range(4):
        slot = jnp.sum(jnp.where(slot_offsets == place, counter, 0))
        matrix = lax.dynamic_index_in_dim(coupling, slot, 0, keepdims=False)
        other = sources[place].reshape(2, vecs * width_x, width_fy)
        prod = jnp.einsum("cri,kio->ckro", other, matrix, preferred_element_type=jnp.float32)
        real_part = prod[0, 0] - prod[1, 1]
        imag_part = prod[0, 1] + prod[1, 0]
        terms.append((matrix, jnp.stack([real_part, imag_part]).reshape(block.shape)))
    last_matrix, last_term = terms[0]
    for _, term in terms[1:]:
        image = image + term
    qfull = block.astype(jnp.float32)
    qr = qfull[0]
    qi = qfull[1]
    wr = image[0]
    wi = image[1]
    num_re = jnp.sum(qr[:, None] * wr[None, :] + qi[:, None] * wi[None, :], axis=(2, 3))
    num_im = jnp.sum(qr[:, None] * wi[None, :] - qi[:, None] * wr[None, :], axis=(2, 3))
    back = jnp.einsum("cro,kio->ckri", block.reshape(2, vecs * width_x, width_fy), last_matrix,
                      preferred_element_type=jnp.float32)
    pull_a = (back[0, 0] + back[1, 1]).reshape(vecs, width_x, width_fy)
    pull_b = (back[1, 0] - back[0, 1]).reshape(vecs, width_x, width_fy)
    s_re = above_two[0].astype(jnp.float32)
    s_im = above_two[1].astype(jnp.float32)
    num_re = num_re + jnp.sum(pull_a[:, None] * s_re[None, :] + pull_b[:, None] * s_im[None, :], axis=(2, 3))
    num_im = num_im + jnp.sum(pull_a[:, None] * s_im[None, :] - pull_b[:, None] * s_re[None, :], axis=(2, 3))
    image = image + last_term
    norms = jnp.sum(qr * qr + qi * qi, axis=(1, 2))
    gathered = exchanged(("harm",), num_re, num_im, norms)
    projected = removed_projections(gathered, image, perturbation)
    return (image.astype(jnp.bfloat16)[None], projected)


def project_kernel(gathered_ref, image_ref, block_ref, out_ref):
    vecs = image_ref.shape[1]
    count, values = gathered_ref.shape
    totals = []
    for j in range(values):
        total = gathered_ref[0, j]
        for i in range(1, count):
            total = total + gathered_ref[i, j]
        totals.append(total)
    block = block_ref[0].astype(jnp.float32)
    for u in range(vecs):
        out_re = image_ref[0, u]
        out_im = image_ref[1, u]
        for v in range(vecs):
            scale = jnp.full((1, 1), totals[2 * vecs * vecs + v] + 1e-06, jnp.float32)
            a = jnp.full((1, 1), totals[v * vecs + u], jnp.float32) / scale
            b = jnp.full((1, 1), totals[vecs * vecs + v * vecs + u], jnp.float32) / scale
            q_re = block[0, v]
            q_im = block[1, v]
            out_re = out_re - (a * q_re - b * q_im)
            out_im = out_im - (a * q_im + b * q_re)
        out_ref[0, 0, u] = out_re.astype(out_ref.dtype)
        out_ref[0, 1, u] = out_im.astype(out_ref.dtype)


def removed_projections(gathered, image, perturbation):
    parts, vecs, width_x, width_fy = image.shape
    rows = 128 if width_x % 128 == 0 else width_x
    return pl.pallas_call(
        project_kernel,
        grid=(width_x // rows,),
        in_specs=[
            pl.BlockSpec(memory_space=pltpu.SMEM),
            pl.BlockSpec((parts, vecs, rows, width_fy), lambda i: (0, 0, i, 0)),
            pl.BlockSpec((1, parts, vecs, rows, width_fy), lambda i: (0, 0, 0, i, 0)),
        ],
        out_specs=pl.BlockSpec((1, parts, vecs, rows, width_fy), lambda i: (0, 0, 0, i, 0)),
        out_shape=jax.ShapeDtypeStruct(perturbation.shape, jnp.bfloat16),
    )(gathered, image, perturbation)


def solution(mesh):
    in_specs = (P(("det", "harm"), None, None, None, None), P(), P(), P(), P(), P(), P("det"))
    out_specs = (
        P(("det", "harm"), None, None, None, None),
        P(("det", "harm"), None, None, None, None),
    )
    return jax.shard_map(body, mesh=mesh, in_specs=in_specs, out_specs=out_specs, check_vma=False)
```

```python
import jax
import jax.numpy as jnp
from jax import lax
from jax.experimental import pallas as pl
from jax.experimental.pallas import tpu as pltpu
from jax.sharding import PartitionSpec as P


def passed_along(value, axis, steps):
    count = lax.axis_size(axis)
    pairs = [(source, (source + steps) % count) for source in range(count)]
    return lax.ppermute(value, axis, pairs)


def exchanged(axes, *parts):
    count = 1
    for axis in axes:
        count = count * lax.axis_size(axis)
    spread = jnp.concatenate([jnp.broadcast_to(part.reshape(1, -1), (count, part.size)) for part in parts], axis=1)
    return lax.all_to_all(spread, axes, 0, 0, tiled=True)


def body(perturbation, coupling, y_operator, x_operator, tile_mask, slot_offsets, detuning):
    block = perturbation[0]
    vecs = block.shape[1]
    width_x = block.shape[2]
    width_fy = block.shape[3]
    ny = y_operator.shape[0]
    harmonics = lax.axis_size("harm")
    position = lax.axis_index("harm")
    tile = width_x // tile_mask.shape[0]
    below_one = passed_along(block, "harm", 1)
    above_one = passed_along(block, "harm", -1)
    below_two = passed_along(below_one, "harm", 1)
    above_two = passed_along(above_one, "harm", -1)
    rows = block.reshape(-1, ny)
    along_y = jnp.dot(rows, y_operator, preferred_element_type=jnp.float32).reshape(block.shape)
    full_mask = jnp.repeat(jnp.repeat(tile_mask, tile, axis=0), tile, axis=1).astype(jnp.bfloat16)
    masked = x_operator * full_mask
    along_x = jnp.einsum("ab,cvbf->cvaf", masked, block, preferred_element_type=jnp.float32)
    centered = (position - harmonics // 2).astype(jnp.float32) + detuning[0]
    lam = -(centered * centered) / (4.0 * harmonics)
    image = lax.optimization_barrier(along_y + along_x + lam * block.astype(jnp.float32))
    sources = (above_two, above_one, below_one, below_two)
    counter = jnp.arange(4, dtype=jnp.int32)
    for place in range(4):
        slot = jnp.sum(jnp.where(slot_offsets == place, counter, 0))
        matrix = lax.dynamic_index_in_dim(coupling, slot, 0, keepdims=False)
        other = sources[place].reshape(2, vecs * width_x, width_fy)
        prod = jnp.einsum("cri,kio->ckro", other, matrix, preferred_element_type=jnp.float32)
        real_part = prod[0, 0] - prod[1, 1]
        imag_part = prod[0, 1] + prod[1, 0]
        image = image + jnp.stack([real_part, imag_part]).reshape(block.shape)
    qfull = block.astype(jnp.float32)
    qr = qfull[0]
    qi = qfull[1]
    wr = image[0]
    wi = image[1]
    num_re = jnp.sum(qr[:, None] * wr[None, :] + qi[:, None] * wi[None, :], axis=(2, 3))
    num_im = jnp.sum(qr[:, None] * wi[None, :] - qi[:, None] * wr[None, :], axis=(2, 3))
    norms = jnp.sum(qr * qr + qi * qi, axis=(1, 2))
    gathered = exchanged(("harm",), num_re, num_im, norms)
    projected = removed_projections(gathered, image, perturbation)
    return (image.astype(jnp.bfloat16)[None], projected)


def project_kernel(gathered_ref, image_ref, block_ref, out_ref):
    vecs = image_ref.shape[1]
    count, values = gathered_ref.shape
    totals = []
    for j in range(values):
        total = gathered_ref[0, j]
        for i in range(1, count):
            total = total + gathered_ref[i, j]
        totals.append(total)
    block = block_ref[0].astype(jnp.float32)
    for u in range(vecs):
        out_re = image_ref[0, u]
        out_im = image_ref[1, u]
        for v in range(vecs):
            scale = jnp.full((1, 1), totals[2 * vecs * vecs + v] + 1e-06, jnp.float32)
            a = jnp.full((1, 1), totals[v * vecs + u], jnp.float32) / scale
            b = jnp.full((1, 1), totals[vecs * vecs + v * vecs + u], jnp.float32) / scale
            q_re = block[0, v]
            q_im = block[1, v]
            out_re = out_re - (a * q_re - b * q_im)
            out_im = out_im - (a * q_im + b * q_re)
        out_ref[0, 0, u] = out_re.astype(out_ref.dtype)
        out_ref[0, 1, u] = out_im.astype(out_ref.dtype)


def removed_projections(gathered, image, perturbation):
    parts, vecs, width_x, width_fy = image.shape
    rows = 128 if width_x % 128 == 0 else width_x
    return pl.pallas_call(
        project_kernel,
        grid=(width_x // rows,),
        in_specs=[
            pl.BlockSpec(memory_space=pltpu.SMEM),
            pl.BlockSpec((parts, vecs, rows, width_fy), lambda i: (0, 0, i, 0)),
            pl.BlockSpec((1, parts, vecs, rows, width_fy), lambda i: (0, 0, 0, i, 0)),
        ],
        out_specs=pl.BlockSpec((1, parts, vecs, rows, width_fy), lambda i: (0, 0, 0, i, 0)),
        out_shape=jax.ShapeDtypeStruct(perturbation.shape, jnp.bfloat16),
    )(gathered, image, perturbation)


def solution(mesh):
    in_specs = (P(("det", "harm"), None, None, None, None), P(), P(), P(), P(), P(), P("det"))
    out_specs = (
        P(("det", "harm"), None, None, None, None),
        P(("det", "harm"), None, None, None, None),
    )
    return jax.shard_map(body, mesh=mesh, in_specs=in_specs, out_specs=out_specs, check_vma=False)
```

```python
import jax
import jax.numpy as jnp
from jax import lax
from jax.experimental import pallas as pl
from jax.experimental.pallas import tpu as pltpu
from jax.sharding import PartitionSpec as P


def passed_along(value, axis, steps):
    count = lax.axis_size(axis)
    pairs = [(source, (source + steps) % count) for source in range(count)]
    return lax.ppermute(value, axis, pairs)


def exchanged(axes, *parts):
    count = 1
    for axis in axes:
        count = count * lax.axis_size(axis)
    spread = jnp.concatenate([jnp.broadcast_to(part.reshape(1, -1), (count, part.size)) for part in parts], axis=1)
    return lax.all_to_all(spread, axes, 0, 0, tiled=True)


def body(perturbation, coupling, y_operator, x_operator, tile_mask, slot_offsets, detuning):
    block = perturbation[0]
    vecs = block.shape[1]
    width_x = block.shape[2]
    width_fy = block.shape[3]
    ny = y_operator.shape[0]
    harmonics = lax.axis_size("harm")
    position = lax.axis_index("harm")
    tile = width_x // tile_mask.shape[0]
    below_one = passed_along(block, "harm", 1)
    above_one = passed_along(block, "harm", -1)
    below_two = passed_along(below_one, "harm", 1)
    above_two = passed_along(above_one, "harm", -1)
    rows = block.reshape(-1, ny)
    along_y = jnp.dot(rows, y_operator, preferred_element_type=jnp.float32).reshape(block.shape)
    full_mask = jnp.repeat(jnp.repeat(tile_mask, tile, axis=0), tile, axis=1).astype(jnp.bfloat16)
    masked = x_operator * full_mask
    along_x = jnp.einsum("ab,cvbf->cvaf", masked, block, preferred_element_type=jnp.float32)
    centered = (position - harmonics // 2).astype(jnp.float32) + detuning[0]
    lam = -(centered * centered) / (4.0 * harmonics)
    image = lax.optimization_barrier(along_y + along_x + lam * block.astype(jnp.float32))
    sources = (above_two, above_one, below_one, below_two)
    counter = jnp.arange(4, dtype=jnp.int32)
    for place in range(4):
        slot = jnp.sum(jnp.where(slot_offsets == place, counter, 0))
        matrix = lax.dynamic_index_in_dim(coupling, slot, 0, keepdims=False)
        other = sources[place].reshape(2, vecs * width_x, width_fy)
        prod = jnp.einsum("cri,kio->ckro", other, matrix, preferred_element_type=jnp.float32)
        real_part = prod[0, 0] - prod[1, 1]
        imag_part = prod[0, 1] + prod[1, 0]
        image = image + jnp.stack([real_part, imag_part]).reshape(block.shape)
    qfull = block.astype(jnp.float32)
    qr = qfull[0]
    qi = qfull[1]
    wr = image[0]
    wi = image[1]
    num_re = jnp.sum(qr[:, None] * wr[None, :] + qi[:, None] * wi[None, :], axis=(2, 3))
    num_im = jnp.sum(qr[:, None] * wi[None, :] - qi[:, None] * wr[None, :], axis=(2, 3))
    norms = jnp.sum(qr * qr + qi * qi, axis=(1, 2))
    gathered = exchanged(("harm",), num_re, num_im, norms)
    rounded, projected = removed_projections(gathered, image, perturbation)
    return (rounded, projected)


def project_kernel(gathered_ref, image_ref, block_ref, rounded_ref, out_ref):
    vecs = image_ref.shape[1]
    count, values = gathered_ref.shape
    totals = []
    for j in range(values):
        total = gathered_ref[0, j]
        for i in range(1, count):
            total = total + gathered_ref[i, j]
        totals.append(total)
    block = block_ref[0].astype(jnp.float32)
    for u in range(vecs):
        out_re = image_ref[0, u]
        out_im = image_ref[1, u]
        rounded_ref[0, 0, u] = out_re.astype(rounded_ref.dtype)
        rounded_ref[0, 1, u] = out_im.astype(rounded_ref.dtype)
        for v in range(vecs):
            scale = jnp.full((1, 1), totals[2 * vecs * vecs + v] + 1e-06, jnp.float32)
            a = jnp.full((1, 1), totals[v * vecs + u], jnp.float32) / scale
            b = jnp.full((1, 1), totals[vecs * vecs + v * vecs + u], jnp.float32) / scale
            q_re = block[0, v]
            q_im = block[1, v]
            out_re = out_re - (a * q_re - b * q_im)
            out_im = out_im - (a * q_im + b * q_re)
        out_ref[0, 0, u] = out_re.astype(out_ref.dtype)
        out_ref[0, 1, u] = out_im.astype(out_ref.dtype)


def removed_projections(gathered, image, perturbation):
    parts, vecs, width_x, width_fy = image.shape
    rows = 128 if width_x % 128 == 0 else width_x
    return pl.pallas_call(
        project_kernel,
        grid=(width_x // rows,),
        in_specs=[
            pl.BlockSpec(memory_space=pltpu.SMEM),
            pl.BlockSpec((parts, vecs, rows, width_fy), lambda i: (0, 0, i, 0)),
            pl.BlockSpec((1, parts, vecs, rows, width_fy), lambda i: (0, 0, 0, i, 0)),
        ],
        out_specs=[
            pl.BlockSpec((1, parts, vecs, rows, width_fy), lambda i: (0, 0, 0, i, 0)),
            pl.BlockSpec((1, parts, vecs, rows, width_fy), lambda i: (0, 0, 0, i, 0)),
        ],
        out_shape=[
            jax.ShapeDtypeStruct(perturbation.shape, jnp.bfloat16),
            jax.ShapeDtypeStruct(perturbation.shape, jnp.bfloat16),
        ],
    )(gathered, image, perturbation)


def solution(mesh):
    in_specs = (P(("det", "harm"), None, None, None, None), P(), P(), P(), P(), P(), P("det"))
    out_specs = (
        P(("det", "harm"), None, None, None, None),
        P(("det", "harm"), None, None, None, None),
    )
    return jax.shard_map(body, mesh=mesh, in_specs=in_specs, out_specs=out_specs, check_vma=False)
```

```python
import jax
import jax.numpy as jnp
from jax import lax
from jax.experimental import pallas as pl
from jax.experimental.pallas import tpu as pltpu
from jax.sharding import PartitionSpec as P


def passed_along(value, axis, steps):
    count = lax.axis_size(axis)
    pairs = [(source, (source + steps) % count) for source in range(count)]
    return lax.ppermute(value, axis, pairs)


def exchanged(axes, *parts):
    count = 1
    for axis in axes:
        count = count * lax.axis_size(axis)
    spread = jnp.concatenate([jnp.broadcast_to(part.reshape(1, -1), (count, part.size)) for part in parts], axis=1)
    return lax.all_to_all(spread, axes, 0, 0, tiled=True)


def body(perturbation, coupling, y_operator, x_operator, tile_mask, slot_offsets, detuning):
    block = perturbation[0]
    vecs = block.shape[1]
    width_x = block.shape[2]
    width_fy = block.shape[3]
    ny = y_operator.shape[0]
    harmonics = lax.axis_size("harm")
    position = lax.axis_index("harm")
    tile = width_x // tile_mask.shape[0]
    below_one = passed_along(block, "harm", 1)
    above_one = passed_along(block, "harm", -1)
    below_two = passed_along(below_one, "harm", 1)
    above_two = passed_along(above_one, "harm", -1)
    rows = block.reshape(-1, ny)
    along_y = jnp.dot(rows, y_operator, preferred_element_type=jnp.float32).reshape(block.shape)
    full_mask = jnp.repeat(jnp.repeat(tile_mask, tile, axis=0), tile, axis=1).astype(jnp.bfloat16)
    masked = x_operator * full_mask
    along_x = jnp.einsum("ab,cvbf->cvaf", masked, block, preferred_element_type=jnp.float32)
    centered = (position - harmonics // 2).astype(jnp.float32) + detuning[0]
    lam = -(centered * centered) / (4.0 * harmonics)
    image = lax.optimization_barrier(along_y + along_x + lam * block.astype(jnp.float32))
    sources = (above_two, above_one, below_one, below_two)
    counter = jnp.arange(4, dtype=jnp.int32)
    for place in range(4):
        slot = jnp.sum(jnp.where(slot_offsets == place, counter, 0))
        matrix = lax.dynamic_index_in_dim(coupling, slot, 0, keepdims=False)
        other = sources[place].reshape(2, vecs * width_x, width_fy)
        prod = jnp.einsum("cri,kio->ckro", other, matrix, preferred_element_type=jnp.float32)
        real_part = prod[0, 0] - prod[1, 1]
        imag_part = prod[0, 1] + prod[1, 0]
        image = image + jnp.stack([real_part, imag_part]).reshape(block.shape)
    qfull = block.astype(jnp.float32)
    qr = qfull[0]
    qi = qfull[1]
    wr = image[0]
    wi = image[1]
    num_re = jnp.sum(qr[:, None] * wr[None, :] + qi[:, None] * wi[None, :], axis=(2, 3))
    num_im = jnp.sum(qr[:, None] * wi[None, :] - qi[:, None] * wr[None, :], axis=(2, 3))
    norms = jnp.sum(qr * qr + qi * qi, axis=(1, 2))
    gathered = exchanged(("harm",), num_re, num_im, norms)
    rounded = rounded_image(image)
    projected = removed_projections(gathered, image, perturbation)
    return (rounded, projected)


def project_kernel(gathered_ref, image_ref, block_ref, out_ref):
    vecs = image_ref.shape[1]
    count, values = gathered_ref.shape
    totals = []
    for j in range(values):
        total = gathered_ref[0, j]
        for i in range(1, count):
            total = total + gathered_ref[i, j]
        totals.append(total)
    block = block_ref[0].astype(jnp.float32)
    for u in range(vecs):
        out_re = image_ref[0, u]
        out_im = image_ref[1, u]
        for v in range(vecs):
            scale = jnp.full((1, 1), totals[2 * vecs * vecs + v] + 1e-06, jnp.float32)
            a = jnp.full((1, 1), totals[v * vecs + u], jnp.float32) / scale
            b = jnp.full((1, 1), totals[vecs * vecs + v * vecs + u], jnp.float32) / scale
            q_re = block[0, v]
            q_im = block[1, v]
            out_re = out_re - (a * q_re - b * q_im)
            out_im = out_im - (a * q_im + b * q_re)
        out_ref[0, 0, u] = out_re.astype(out_ref.dtype)
        out_ref[0, 1, u] = out_im.astype(out_ref.dtype)


def removed_projections(gathered, image, perturbation):
    parts, vecs, width_x, width_fy = image.shape
    rows = 128 if width_x % 128 == 0 else width_x
    return pl.pallas_call(
        project_kernel,
        grid=(width_x // rows,),
        in_specs=[
            pl.BlockSpec(memory_space=pltpu.SMEM),
            pl.BlockSpec((parts, vecs, rows, width_fy), lambda i: (0, 0, i, 0)),
            pl.BlockSpec((1, parts, vecs, rows, width_fy), lambda i: (0, 0, 0, i, 0)),
        ],
        out_specs=pl.BlockSpec((1, parts, vecs, rows, width_fy), lambda i: (0, 0, 0, i, 0)),
        out_shape=jax.ShapeDtypeStruct(perturbation.shape, jnp.bfloat16),
    )(gathered, image, perturbation)


def round_kernel(image_ref, out_ref):
    out_ref[0] = image_ref[...].astype(out_ref.dtype)


def rounded_image(image):
    parts, vecs, width_x, width_fy = image.shape
    rows = 128 if width_x % 128 == 0 else width_x
    return pl.pallas_call(
        round_kernel,
        grid=(width_x // rows,),
        in_specs=[pl.BlockSpec((parts, vecs, rows, width_fy), lambda i: (0, 0, i, 0))],
        out_specs=pl.BlockSpec((1, parts, vecs, rows, width_fy), lambda i: (0, 0, 0, i, 0)),
        out_shape=jax.ShapeDtypeStruct((1,) + image.shape, jnp.bfloat16),
    )(image)


def solution(mesh):
    in_specs = (P(("det", "harm"), None, None, None, None), P(), P(), P(), P(), P(), P("det"))
    out_specs = (
        P(("det", "harm"), None, None, None, None),
        P(("det", "harm"), None, None, None, None),
    )
    return jax.shard_map(body, mesh=mesh, in_specs=in_specs, out_specs=out_specs, check_vma=False)
```

```python
import jax
import jax.numpy as jnp
from jax import lax
from jax.experimental import pallas as pl
from jax.experimental.pallas import tpu as pltpu
from jax.sharding import PartitionSpec as P


def passed_along(value, axis, steps):
    count = lax.axis_size(axis)
    pairs = [(source, (source + steps) % count) for source in range(count)]
    return lax.ppermute(value, axis, pairs)


def exchanged(axes, *parts):
    count = 1
    for axis in axes:
        count = count * lax.axis_size(axis)
    spread = jnp.concatenate([jnp.broadcast_to(part.reshape(1, -1), (count, part.size)) for part in parts], axis=1)
    return lax.all_to_all(spread, axes, 0, 0, tiled=True)


def body(perturbation, coupling, y_operator, x_operator, tile_mask, slot_offsets, detuning):
    block = perturbation[0]
    vecs = block.shape[1]
    width_x = block.shape[2]
    width_fy = block.shape[3]
    ny = y_operator.shape[0]
    harmonics = lax.axis_size("harm")
    position = lax.axis_index("harm")
    tile = width_x // tile_mask.shape[0]
    below_one = passed_along(block, "harm", 1)
    above_one = passed_along(block, "harm", -1)
    below_two = passed_along(below_one, "harm", 1)
    above_two = passed_along(above_one, "harm", -1)
    rows = block.reshape(-1, ny)
    along_y = jnp.dot(rows, y_operator, preferred_element_type=jnp.float32).reshape(block.shape)
    full_mask = jnp.repeat(jnp.repeat(tile_mask, tile, axis=0), tile, axis=1).astype(jnp.bfloat16)
    masked = x_operator * full_mask
    along_x = jnp.einsum("ab,cvbf->cvaf", masked, block, preferred_element_type=jnp.float32)
    centered = (position - harmonics // 2).astype(jnp.float32) + detuning[0]
    lam = -(centered * centered) / (4.0 * harmonics)
    image = lax.optimization_barrier(along_y + along_x + lam * block.astype(jnp.float32))
    sources = (above_two, above_one, below_one, below_two)
    counter = jnp.arange(4, dtype=jnp.int32)
    for place in range(4):
        slot = jnp.sum(jnp.where(slot_offsets == place, counter, 0))
        matrix = lax.dynamic_index_in_dim(coupling, slot, 0, keepdims=False)
        other = sources[place].reshape(2, vecs * width_x, width_fy)
        prod = jnp.einsum("cri,kio->ckro", other, matrix, preferred_element_type=jnp.float32)
        real_part = prod[0, 0] - prod[1, 1]
        imag_part = prod[0, 1] + prod[1, 0]
        image = image + jnp.stack([real_part, imag_part]).reshape(block.shape)
    qfull = block.astype(jnp.float32)
    qr = qfull[0]
    qi = qfull[1]
    wr = image[0]
    wi = image[1]
    groups = 8 if width_x % 8 == 0 else 1
    split = (vecs, vecs, groups, width_x // groups, width_fy)
    part_re = jnp.sum((qr[:, None] * wr[None, :] + qi[:, None] * wi[None, :]).reshape(split), axis=(3, 4))
    part_im = jnp.sum((qr[:, None] * wi[None, :] - qi[:, None] * wr[None, :]).reshape(split), axis=(3, 4))
    part_re, part_im = lax.optimization_barrier((part_re, part_im))
    num_re = jnp.sum(part_re, axis=2)
    num_im = jnp.sum(part_im, axis=2)
    norms = jnp.sum(qr * qr + qi * qi, axis=(1, 2))
    gathered = exchanged(("harm",), num_re, num_im, norms)
    rounded, projected = removed_projections(gathered, image, perturbation)
    return (rounded, projected)


def project_kernel(gathered_ref, image_ref, block_ref, rounded_ref, out_ref):
    vecs = image_ref.shape[1]
    count, values = gathered_ref.shape
    totals = []
    for j in range(values):
        total = gathered_ref[0, j]
        for i in range(1, count):
            total = total + gathered_ref[i, j]
        totals.append(total)
    block = block_ref[0].astype(jnp.float32)
    for u in range(vecs):
        out_re = image_ref[0, u]
        out_im = image_ref[1, u]
        rounded_ref[0, 0, u] = out_re.astype(rounded_ref.dtype)
        rounded_ref[0, 1, u] = out_im.astype(rounded_ref.dtype)
        for v in range(vecs):
            scale = jnp.full((1, 1), totals[2 * vecs * vecs + v] + 1e-06, jnp.float32)
            a = jnp.full((1, 1), totals[v * vecs + u], jnp.float32) / scale
            b = jnp.full((1, 1), totals[vecs * vecs + v * vecs + u], jnp.float32) / scale
            q_re = block[0, v]
            q_im = block[1, v]
            out_re = out_re - (a * q_re - b * q_im)
            out_im = out_im - (a * q_im + b * q_re)
        out_ref[0, 0, u] = out_re.astype(out_ref.dtype)
        out_ref[0, 1, u] = out_im.astype(out_ref.dtype)


def removed_projections(gathered, image, perturbation):
    parts, vecs, width_x, width_fy = image.shape
    rows = 128 if width_x % 128 == 0 else width_x
    return pl.pallas_call(
        project_kernel,
        grid=(width_x // rows,),
        in_specs=[
            pl.BlockSpec(memory_space=pltpu.SMEM),
            pl.BlockSpec((parts, vecs, rows, width_fy), lambda i: (0, 0, i, 0)),
            pl.BlockSpec((1, parts, vecs, rows, width_fy), lambda i: (0, 0, 0, i, 0)),
        ],
        out_specs=[
            pl.BlockSpec((1, parts, vecs, rows, width_fy), lambda i: (0, 0, 0, i, 0)),
            pl.BlockSpec((1, parts, vecs, rows, width_fy), lambda i: (0, 0, 0, i, 0)),
        ],
        out_shape=[
            jax.ShapeDtypeStruct(perturbation.shape, jnp.bfloat16),
            jax.ShapeDtypeStruct(perturbation.shape, jnp.bfloat16),
        ],
    )(gathered, image, perturbation)


def solution(mesh):
    in_specs = (P(("det", "harm"), None, None, None, None), P(), P(), P(), P(), P(), P("det"))
    out_specs = (
        P(("det", "harm"), None, None, None, None),
        P(("det", "harm"), None, None, None, None),
    )
    return jax.shard_map(body, mesh=mesh, in_specs=in_specs, out_specs=out_specs, check_vma=False)
```

```python
import jax
import jax.numpy as jnp
from jax import lax
from jax.experimental import pallas as pl
from jax.experimental.pallas import tpu as pltpu
from jax.sharding import PartitionSpec as P


def passed_along(value, axis, steps):
    count = lax.axis_size(axis)
    pairs = [(source, (source + steps) % count) for source in range(count)]
    return lax.ppermute(value, axis, pairs)


def exchanged(axes, *parts):
    count = 1
    for axis in axes:
        count = count * lax.axis_size(axis)
    spread = jnp.concatenate([jnp.broadcast_to(part.reshape(1, -1), (count, part.size)) for part in parts], axis=1)
    return lax.all_to_all(spread, axes, 0, 0, tiled=True)


def body(perturbation, coupling, y_operator, x_operator, tile_mask, slot_offsets, detuning):
    block = perturbation[0]
    vecs = block.shape[1]
    width_x = block.shape[2]
    width_fy = block.shape[3]
    ny = y_operator.shape[0]
    harmonics = lax.axis_size("harm")
    position = lax.axis_index("harm")
    tile = width_x // tile_mask.shape[0]
    below_one = passed_along(block, "harm", 1)
    above_one = passed_along(block, "harm", -1)
    below_two = passed_along(below_one, "harm", 1)
    above_two = passed_along(above_one, "harm", -1)
    rows = block.reshape(-1, ny)
    along_y = jnp.dot(rows, y_operator, preferred_element_type=jnp.float32).reshape(block.shape)
    full_mask = jnp.repeat(jnp.repeat(tile_mask, tile, axis=0), tile, axis=1).astype(jnp.bfloat16)
    masked = x_operator * full_mask
    along_x = jnp.einsum("ab,cvbf->cvaf", masked, block, preferred_element_type=jnp.float32)
    centered = (position - harmonics // 2).astype(jnp.float32) + detuning[0]
    lam = -(centered * centered) / (4.0 * harmonics)
    image = lax.optimization_barrier(along_y + along_x + lam * block.astype(jnp.float32))
    sources = (above_two, above_one, below_one, below_two)
    counter = jnp.arange(4, dtype=jnp.int32)
    for place in range(4):
        slot = jnp.sum(jnp.where(slot_offsets == place, counter, 0))
        matrix = lax.dynamic_index_in_dim(coupling, slot, 0, keepdims=False)
        other = sources[place].reshape(2, vecs * width_x, width_fy)
        prod = jnp.einsum("cri,kio->ckro", other, matrix, preferred_element_type=jnp.float32)
        real_part = prod[0, 0] - prod[1, 1]
        imag_part = prod[0, 1] + prod[1, 0]
        image = image + jnp.stack([real_part, imag_part]).reshape(block.shape)
    qfull = block.astype(jnp.float32)
    qr = qfull[0]
    qi = qfull[1]
    wr = image[0]
    wi = image[1]
    groups = 8 if width_x % 8 == 0 else 1
    split = (vecs, vecs, groups, width_x // groups, width_fy)
    part_re = jnp.sum((qr[:, None] * wr[None, :] + qi[:, None] * wi[None, :]).reshape(split), axis=(3, 4))
    part_im = jnp.sum((qr[:, None] * wi[None, :] - qi[:, None] * wr[None, :]).reshape(split), axis=(3, 4))
    part_re, part_im = lax.optimization_barrier((part_re, part_im))
    num_re = jnp.sum(part_re, axis=2)
    num_im = jnp.sum(part_im, axis=2)
    norms = jnp.sum(qr * qr + qi * qi, axis=(1, 2))
    gathered = exchanged(("harm",), num_re, num_im, norms)
    totals = jnp.sum(gathered, axis=0)
    square = vecs * vecs
    h_re = (totals[:square].reshape(vecs, vecs) / (totals[2 * square:] + 1e-06)[:, None])
    h_im = (totals[square:2 * square].reshape(vecs, vecs) / (totals[2 * square:] + 1e-06)[:, None])
    turned = jnp.stack([-qi, qr])
    projected = image
    for vec in range(vecs):
        projected = projected - (h_re[vec, :, None, None] * qfull[:, vec][:, None]
                                 + h_im[vec, :, None, None] * turned[:, vec][:, None])
    return (image.astype(jnp.bfloat16)[None], projected.astype(jnp.bfloat16)[None])


def project_kernel(gathered_ref, image_ref, block_ref, rounded_ref, out_ref):
    vecs = image_ref.shape[1]
    count, values = gathered_ref.shape
    totals = []
    for j in range(values):
        total = gathered_ref[0, j]
        for i in range(1, count):
            total = total + gathered_ref[i, j]
        totals.append(total)
    block = block_ref[0].astype(jnp.float32)
    for u in range(vecs):
        out_re = image_ref[0, u]
        out_im = image_ref[1, u]
        rounded_ref[0, 0, u] = out_re.astype(rounded_ref.dtype)
        rounded_ref[0, 1, u] = out_im.astype(rounded_ref.dtype)
        for v in range(vecs):
            scale = jnp.full((1, 1), totals[2 * vecs * vecs + v] + 1e-06, jnp.float32)
            a = jnp.full((1, 1), totals[v * vecs + u], jnp.float32) / scale
            b = jnp.full((1, 1), totals[vecs * vecs + v * vecs + u], jnp.float32) / scale
            q_re = block[0, v]
            q_im = block[1, v]
            out_re = out_re - (a * q_re - b * q_im)
            out_im = out_im - (a * q_im + b * q_re)
        out_ref[0, 0, u] = out_re.astype(out_ref.dtype)
        out_ref[0, 1, u] = out_im.astype(out_ref.dtype)


def removed_projections(gathered, image, perturbation):
    parts, vecs, width_x, width_fy = image.shape
    rows = 128 if width_x % 128 == 0 else width_x
    return pl.pallas_call(
        project_kernel,
        grid=(width_x // rows,),
        in_specs=[
            pl.BlockSpec(memory_space=pltpu.SMEM),
            pl.BlockSpec((parts, vecs, rows, width_fy), lambda i: (0, 0, i, 0)),
            pl.BlockSpec((1, parts, vecs, rows, width_fy), lambda i: (0, 0, 0, i, 0)),
        ],
        out_specs=[
            pl.BlockSpec((1, parts, vecs, rows, width_fy), lambda i: (0, 0, 0, i, 0)),
            pl.BlockSpec((1, parts, vecs, rows, width_fy), lambda i: (0, 0, 0, i, 0)),
        ],
        out_shape=[
            jax.ShapeDtypeStruct(perturbation.shape, jnp.bfloat16),
            jax.ShapeDtypeStruct(perturbation.shape, jnp.bfloat16),
        ],
    )(gathered, image, perturbation)


def solution(mesh):
    in_specs = (P(("det", "harm"), None, None, None, None), P(), P(), P(), P(), P(), P("det"))
    out_specs = (
        P(("det", "harm"), None, None, None, None),
        P(("det", "harm"), None, None, None, None),
    )
    return jax.shard_map(body, mesh=mesh, in_specs=in_specs, out_specs=out_specs, check_vma=False)
```

```python
import jax
import jax.numpy as jnp
from jax import lax
from jax.experimental import pallas as pl
from jax.experimental.pallas import tpu as pltpu
from jax.sharding import PartitionSpec as P


def passed_along(value, axis, steps):
    count = lax.axis_size(axis)
    pairs = [(source, (source + steps) % count) for source in range(count)]
    return lax.ppermute(value, axis, pairs)


def exchanged(axes, *parts):
    count = 1
    for axis in axes:
        count = count * lax.axis_size(axis)
    spread = jnp.concatenate([jnp.broadcast_to(part.reshape(1, -1), (count, part.size)) for part in parts], axis=1)
    return lax.all_to_all(spread, axes, 0, 0, tiled=True)


def body(perturbation, coupling, y_operator, x_operator, tile_mask, slot_offsets, detuning):
    block = perturbation[0]
    vecs = block.shape[1]
    width_x = block.shape[2]
    width_fy = block.shape[3]
    ny = y_operator.shape[0]
    harmonics = lax.axis_size("harm")
    position = lax.axis_index("harm")
    tile = width_x // tile_mask.shape[0]
    below_one = passed_along(block, "harm", 1)
    above_one = passed_along(block, "harm", -1)
    below_two = passed_along(below_one, "harm", 1)
    above_two = passed_along(above_one, "harm", -1)
    rows = block.reshape(-1, ny)
    along_y = jnp.dot(rows, y_operator, preferred_element_type=jnp.float32).reshape(block.shape)
    full_mask = jnp.repeat(jnp.repeat(tile_mask, tile, axis=0), tile, axis=1).astype(jnp.bfloat16)
    masked = x_operator * full_mask
    along_x = jnp.einsum("ab,cvbf->cvaf", masked, block, preferred_element_type=jnp.float32)
    centered = (position - harmonics // 2).astype(jnp.float32) + detuning[0]
    lam = -(centered * centered) / (4.0 * harmonics)
    image = lax.optimization_barrier(along_y + along_x + lam * block.astype(jnp.float32))
    sources = (above_two, above_one, below_one, below_two)
    counter = jnp.arange(4, dtype=jnp.int32)
    for place in range(4):
        slot = jnp.sum(jnp.where(slot_offsets == place, counter, 0))
        matrix = lax.dynamic_index_in_dim(coupling, slot, 0, keepdims=False)
        other = sources[place].reshape(2, vecs * width_x, width_fy)
        prod = jnp.einsum("cri,kio->ckro", other, matrix, preferred_element_type=jnp.float32)
        real_part = prod[0, 0] - prod[1, 1]
        imag_part = prod[0, 1] + prod[1, 0]
        image = image + jnp.stack([real_part, imag_part]).reshape(block.shape)
    qfull = block.astype(jnp.float32)
    qr = qfull[0]
    qi = qfull[1]
    wr = image[0]
    wi = image[1]
    groups = 32 if width_x % 32 == 0 else 1
    split = (vecs, vecs, groups, width_x // groups, width_fy)
    part_re = jnp.sum((qr[:, None] * wr[None, :] + qi[:, None] * wi[None, :]).reshape(split), axis=(3, 4))
    part_im = jnp.sum((qr[:, None] * wi[None, :] - qi[:, None] * wr[None, :]).reshape(split), axis=(3, 4))
    part_re, part_im = lax.optimization_barrier((part_re, part_im))
    num_re = jnp.sum(part_re, axis=2)
    num_im = jnp.sum(part_im, axis=2)
    norms = jnp.sum(qr * qr + qi * qi, axis=(1, 2))
    gathered = exchanged(("harm",), num_re, num_im, norms)
    rounded, projected = removed_projections(gathered, image, perturbation)
    return (rounded, projected)


def project_kernel(gathered_ref, image_ref, block_ref, rounded_ref, out_ref):
    vecs = image_ref.shape[1]
    count, values = gathered_ref.shape
    totals = []
    for j in range(values):
        total = gathered_ref[0, j]
        for i in range(1, count):
            total = total + gathered_ref[i, j]
        totals.append(total)
    block = block_ref[0].astype(jnp.float32)
    for u in range(vecs):
        out_re = image_ref[0, u]
        out_im = image_ref[1, u]
        rounded_ref[0, 0, u] = out_re.astype(rounded_ref.dtype)
        rounded_ref[0, 1, u] = out_im.astype(rounded_ref.dtype)
        for v in range(vecs):
            scale = jnp.full((1, 1), totals[2 * vecs * vecs + v] + 1e-06, jnp.float32)
            a = jnp.full((1, 1), totals[v * vecs + u], jnp.float32) / scale
            b = jnp.full((1, 1), totals[vecs * vecs + v * vecs + u], jnp.float32) / scale
            q_re = block[0, v]
            q_im = block[1, v]
            out_re = out_re - (a * q_re - b * q_im)
            out_im = out_im - (a * q_im + b * q_re)
        out_ref[0, 0, u] = out_re.astype(out_ref.dtype)
        out_ref[0, 1, u] = out_im.astype(out_ref.dtype)


def removed_projections(gathered, image, perturbation):
    parts, vecs, width_x, width_fy = image.shape
    rows = 128 if width_x % 128 == 0 else width_x
    return pl.pallas_call(
        project_kernel,
        grid=(width_x // rows,),
        in_specs=[
            pl.BlockSpec(memory_space=pltpu.SMEM),
            pl.BlockSpec((parts, vecs, rows, width_fy), lambda i: (0, 0, i, 0)),
            pl.BlockSpec((1, parts, vecs, rows, width_fy), lambda i: (0, 0, 0, i, 0)),
        ],
        out_specs=[
            pl.BlockSpec((1, parts, vecs, rows, width_fy), lambda i: (0, 0, 0, i, 0)),
            pl.BlockSpec((1, parts, vecs, rows, width_fy), lambda i: (0, 0, 0, i, 0)),
        ],
        out_shape=[
            jax.ShapeDtypeStruct(perturbation.shape, jnp.bfloat16),
            jax.ShapeDtypeStruct(perturbation.shape, jnp.bfloat16),
        ],
    )(gathered, image, perturbation)


def solution(mesh):
    in_specs = (P(("det", "harm"), None, None, None, None), P(), P(), P(), P(), P(), P("det"))
    out_specs = (
        P(("det", "harm"), None, None, None, None),
        P(("det", "harm"), None, None, None, None),
    )
    return jax.shard_map(body, mesh=mesh, in_specs=in_specs, out_specs=out_specs, check_vma=False)
```

```python
import jax
import jax.numpy as jnp
from jax import lax
from jax.experimental import pallas as pl
from jax.experimental.pallas import tpu as pltpu
from jax.sharding import PartitionSpec as P


def passed_along(value, axis, steps):
    count = lax.axis_size(axis)
    pairs = [(source, (source + steps) % count) for source in range(count)]
    return lax.ppermute(value, axis, pairs)


def exchanged(axes, *parts):
    count = 1
    for axis in axes:
        count = count * lax.axis_size(axis)
    spread = jnp.concatenate([jnp.broadcast_to(part.reshape(1, -1), (count, part.size)) for part in parts], axis=1)
    return lax.all_to_all(spread, axes, 0, 0, tiled=True)


def body(perturbation, coupling, y_operator, x_operator, tile_mask, slot_offsets, detuning):
    block = perturbation[0]
    vecs = block.shape[1]
    width_x = block.shape[2]
    width_fy = block.shape[3]
    ny = y_operator.shape[0]
    harmonics = lax.axis_size("harm")
    position = lax.axis_index("harm")
    tile = width_x // tile_mask.shape[0]
    below_one = passed_along(block, "harm", 1)
    above_one = passed_along(block, "harm", -1)
    below_two = passed_along(below_one, "harm", 1)
    above_two = passed_along(above_one, "harm", -1)
    rows = block.reshape(-1, ny)
    along_y = jnp.dot(rows, y_operator, preferred_element_type=jnp.float32).reshape(block.shape)
    full_mask = jnp.repeat(jnp.repeat(tile_mask, tile, axis=0), tile, axis=1).astype(jnp.bfloat16)
    masked = x_operator * full_mask
    along_x = jnp.einsum("ab,cvbf->cvaf", masked, block, preferred_element_type=jnp.float32)
    centered = (position - harmonics // 2).astype(jnp.float32) + detuning[0]
    lam = -(centered * centered) / (4.0 * harmonics)
    local = lax.optimization_barrier(along_y + along_x + lam * block.astype(jnp.float32))
    qfull = block.astype(jnp.float32)
    qr = qfull[0]
    qi = qfull[1]

    def products(part):
        part_re = jnp.sum(qr[:, None] * part[0][None, :] + qi[:, None] * part[1][None, :], axis=(2, 3))
        part_im = jnp.sum(qr[:, None] * part[1][None, :] - qi[:, None] * part[0][None, :], axis=(2, 3))
        return part_re, part_im

    local_re, local_im = lax.optimization_barrier(products(local))
    sources = (above_two, above_one, below_one, below_two)
    counter = jnp.arange(4, dtype=jnp.int32)
    coupled = None
    for place in range(4):
        slot = jnp.sum(jnp.where(slot_offsets == place, counter, 0))
        matrix = lax.dynamic_index_in_dim(coupling, slot, 0, keepdims=False)
        other = sources[place].reshape(2, vecs * width_x, width_fy)
        prod = jnp.einsum("cri,kio->ckro", other, matrix, preferred_element_type=jnp.float32)
        real_part = prod[0, 0] - prod[1, 1]
        imag_part = prod[0, 1] + prod[1, 0]
        term = jnp.stack([real_part, imag_part]).reshape(block.shape)
        coupled = term if coupled is None else coupled + term
    coupled_re, coupled_im = products(coupled)
    norms = jnp.sum(qr * qr + qi * qi, axis=(1, 2))
    gathered = exchanged(("harm",), local_re + coupled_re, local_im + coupled_im, norms)
    rounded, projected = removed_projections(gathered, local, coupled, perturbation)
    return (rounded, projected)


def project_kernel(gathered_ref, image_ref, coupled_ref, block_ref, rounded_ref, out_ref):
    vecs = image_ref.shape[1]
    count, values = gathered_ref.shape
    totals = []
    for j in range(values):
        total = gathered_ref[0, j]
        for i in range(1, count):
            total = total + gathered_ref[i, j]
        totals.append(total)
    block = block_ref[0].astype(jnp.float32)
    for u in range(vecs):
        out_re = image_ref[0, u] + coupled_ref[0, u]
        out_im = image_ref[1, u] + coupled_ref[1, u]
        rounded_ref[0, 0, u] = out_re.astype(rounded_ref.dtype)
        rounded_ref[0, 1, u] = out_im.astype(rounded_ref.dtype)
        for v in range(vecs):
            scale = jnp.full((1, 1), totals[2 * vecs * vecs + v] + 1e-06, jnp.float32)
            a = jnp.full((1, 1), totals[v * vecs + u], jnp.float32) / scale
            b = jnp.full((1, 1), totals[vecs * vecs + v * vecs + u], jnp.float32) / scale
            q_re = block[0, v]
            q_im = block[1, v]
            out_re = out_re - (a * q_re - b * q_im)
            out_im = out_im - (a * q_im + b * q_re)
        out_ref[0, 0, u] = out_re.astype(out_ref.dtype)
        out_ref[0, 1, u] = out_im.astype(out_ref.dtype)


def removed_projections(gathered, image, coupled, perturbation):
    parts, vecs, width_x, width_fy = image.shape
    rows = 128 if width_x % 128 == 0 else width_x
    return pl.pallas_call(
        project_kernel,
        grid=(width_x // rows,),
        in_specs=[
            pl.BlockSpec(memory_space=pltpu.SMEM),
            pl.BlockSpec((parts, vecs, rows, width_fy), lambda i: (0, 0, i, 0)),
            pl.BlockSpec((parts, vecs, rows, width_fy), lambda i: (0, 0, i, 0)),
            pl.BlockSpec((1, parts, vecs, rows, width_fy), lambda i: (0, 0, 0, i, 0)),
        ],
        out_specs=[
            pl.BlockSpec((1, parts, vecs, rows, width_fy), lambda i: (0, 0, 0, i, 0)),
            pl.BlockSpec((1, parts, vecs, rows, width_fy), lambda i: (0, 0, 0, i, 0)),
        ],
        out_shape=[
            jax.ShapeDtypeStruct(perturbation.shape, jnp.bfloat16),
            jax.ShapeDtypeStruct(perturbation.shape, jnp.bfloat16),
        ],
    )(gathered, image, coupled, perturbation)


def solution(mesh):
    in_specs = (P(("det", "harm"), None, None, None, None), P(), P(), P(), P(), P(), P("det"))
    out_specs = (
        P(("det", "harm"), None, None, None, None),
        P(("det", "harm"), None, None, None, None),
    )
    return jax.shard_map(body, mesh=mesh, in_specs=in_specs, out_specs=out_specs, check_vma=False)
```
